256 devices in a mesh: prompt: 16 (over x_hi, z), resp: 8 (over x_lo, y), head: 2 (over core).
Axes of the slice: x: 4 (x_hi: 2, x_lo: 2; x = x_hi * 2 + x_lo), y: 4, z: 8, core: 2. Of those that a mesh axis runs over, the one named last changes fastest.
Arguments:
- prompt_q: bfloat16 [8, 1024, 4, 512], P('resp', 'prompt', None, 'head'), may hold values from -250 to 250
- prompt_kv: bfloat16 [2, 8, 1024, 512], P(None, 'resp', 'prompt'), may hold values from -8 to 8
- prompt_grad: bfloat16 [8, 1024, 4, 512], P('resp', 'prompt', None, 'head'), may hold values from -6 to 6
- resp_q: bfloat16 [16, 8, 8, 64, 4, 512], P('prompt', 'resp', None, None, None, 'head'), may hold values from -250 to 250
- resp_kv: bfloat16 [2, 16, 8, 8, 64, 512], P(None, 'prompt', 'resp'), may hold values from -6 to 6
- resp_grad: bfloat16 [16, 8, 8, 64, 4, 512], P('prompt', 'resp', None, None, None, 'head'), may hold values from -6 to 6
- resp_prompt: int32 [16, 8, 8], P('prompt', 'resp'), may hold values from 0 to 7, as said below
Outputs:
- prompt_out: bfloat16 [8, 1024, 4, 512], P('resp', 'prompt', None, 'head')
- prompt_dq: bfloat16 [8, 1024, 4, 512], P('resp', 'prompt', None, 'head')
- prompt_dkv: bfloat16 [2, 8, 1024, 512], P(None, 'resp', 'prompt', 'head')
- resp_out: bfloat16 [16, 8, 8, 64, 4, 512], P('prompt', 'resp', None, None, None, 'head')
- resp_dq: bfloat16 [16, 8, 8, 64, 4, 512], P('prompt', 'resp', None, None, None, 'head')
- resp_dkv: bfloat16 [2, 16, 8, 8, 64, 512], P(None, 'prompt', 'resp', None, None, 'head')
The draws below stay inside these ranges and needn't reach their ends.
Inputs may be any that keep to these rules, and one draw needn't show every extreme that they name: `resp_prompt`: entry [p, r, j] is the prompt of response j held at prompt index p and resp index r; each row of 8 entries names every prompt once.
All inputs are finite; a program needn't handle non-finite values.
Results may differ from the reference program's by a relative error of at most 0.0095.
Values may be sent and summed in bfloat16 or wider, within the bound.
No kernel may reach another device: no remote copies, remote signals or barrier semaphores. Data moves between devices by JAX's collectives and lax.ppermute only.
A program may use at most 128 MiB of HBM per device.

```python
import math
import jax
import jax.numpy as jnp
from jax import lax

HD = 128
KVH = 4
GROUP = 4
RLEN = 64
PROMPTS = 8
PLEN = 1024
N_PROMPT = 16
N_RESP = 8


def shared_keys(key):
    return jax.random.normal(jax.random.fold_in(key, 11), (2, PROMPTS, PLEN, KVH * HD), jnp.float32)


def placement(key):
    folded = jax.random.fold_in(key, 7)
    row_keys = jax.random.split(folded, N_PROMPT * N_RESP)

    def one_row(row_key):
        return jax.random.permutation(row_key, N_RESP)
    return jax.vmap(one_row)(row_keys).reshape(N_PROMPT, N_RESP, N_RESP).astype(jnp.int32)


def draw_prompt_kv(key, part):
    return shared_keys(key).astype(jnp.bfloat16)


def draw_resp_prompt(key, part):
    return placement(key)


def draw_prompt_q(key, part):
    drawn = jax.random.normal(jax.random.fold_in(key, 13), (PROMPTS, PLEN, KVH, GROUP, HD), jnp.float32)
    return drawn.reshape(PROMPTS, PLEN, KVH, GROUP * HD).astype(jnp.bfloat16)


def draw_resp_q(key, part):
    drawn = jax.random.normal(jax.random.fold_in(key, 17), (N_PROMPT, N_RESP, N_RESP, RLEN, KVH, GROUP, HD), jnp.float32)
    return drawn.reshape(N_PROMPT, N_RESP, N_RESP, RLEN, KVH, GROUP * HD).astype(jnp.bfloat16)


def steps_of(own_key, dims, shards, low, high):
    gain = 1.0
    for dim, blocks in shards:
        heights = jax.random.uniform(jax.random.fold_in(jax.random.fold_in(own_key, 6), dim), (blocks,), jnp.float32, low / len(shards), high / len(shards))
        gain = gain * jnp.repeat(jnp.exp(heights), dims[dim] // blocks).reshape((-1,) + (1,) * (len(dims) - 1 - dim))
    return gain


def gaussian(key, shape, spread, most, cuts=(), kind=jnp.bfloat16):
    loudness = steps_of(key, shape, cuts, -0.22, 0.18) if cuts else 1.0
    result = jax.random.normal(key, shape, jnp.float32) * spread * loudness
    return jnp.minimum(jnp.maximum(result, -most), most).astype(kind)


def setup_inputs(seed: int = 0) -> dict:
    streams_of = jax.random.split(jax.random.key(seed), 8)
    prompt_q = draw_prompt_q(jax.random.fold_in(streams_of[7], 71), 0)
    prompt_kv = draw_prompt_kv(jax.random.fold_in(streams_of[7], 71), 0)
    prompt_grad = gaussian(streams_of[2], (PROMPTS, PLEN, KVH, GROUP * HD), 1.0, 6.0, ((0, 8), (1, 16), (3, 2)))
    resp_q = draw_resp_q(jax.random.fold_in(streams_of[7], 71), 0)
    resp_kv = gaussian(streams_of[4], (2, N_PROMPT, N_RESP, N_RESP, RLEN, KVH * HD), 1.0, 6.0, ((1, 16), (2, 8)))
    resp_grad = gaussian(streams_of[5], (N_PROMPT, N_RESP, N_RESP, RLEN, KVH, GROUP * HD), 1.0, 6.0, ((0, 16), (1, 8), (5, 2)))
    resp_prompt = draw_resp_prompt(jax.random.fold_in(streams_of[7], 71), 0)
    return {"prompt_q": prompt_q, "prompt_kv": prompt_kv, "prompt_grad": prompt_grad, "resp_q": resp_q, "resp_kv": resp_kv, "resp_grad": resp_grad, "resp_prompt": resp_prompt}


def rounded(values_in):
    return lax.optimization_barrier(values_in.astype(jnp.bfloat16)).astype(jnp.float32)

def attend(queries, keys_in, values_in, cotangent, allowed):
    scale = 1.0 / math.sqrt(HD)
    query_f = queries.astype(jnp.float32)
    key_f = keys_in.astype(jnp.float32)
    value_f = values_in.astype(jnp.float32)
    grad_f = cotangent.astype(jnp.float32)
    scores = jnp.einsum('brkgd,bnkd->bkgrn', query_f, key_f) * scale
    scores = jnp.where(allowed, scores, -1e+30)
    row_max = lax.optimization_barrier(jnp.max(scores, axis=-1, keepdims=True))
    totals = lax.optimization_barrier(jnp.sum(jnp.exp(scores - row_max), axis=-1, keepdims=True))
    log_total = row_max + jnp.log(totals)
    probabilities = jnp.exp(scores - log_total)
    weights = rounded(probabilities)
    output = jnp.einsum('bkgrn,bnkd->brkgd', weights, value_f).astype(jnp.bfloat16)
    row_delta = jnp.einsum('brkgd,brkgd->bkgr', grad_f, output.astype(jnp.float32))
    dprobs = jnp.einsum('brkgd,bnkd->bkgrn', grad_f, value_f)
    dscores = rounded(probabilities * (dprobs - row_delta[..., None]))
    dquery = jnp.einsum('bkgrn,bnkd->brkgd', dscores, key_f) * scale
    dkeys = jnp.einsum('bkgrn,brkgd->bnkd', dscores, query_f) * scale
    dvalues = jnp.einsum('bkgrn,brkgd->bnkd', weights, grad_f)
    return (output, dquery, dkeys, dvalues)

def reference(prompt_q, prompt_kv, prompt_grad, resp_q, resp_kv, resp_grad, resp_prompt):
    positions = jnp.arange(PLEN)
    causal = positions[None, :] <= positions[:, None]
    out_list, dq_list, grad_list = ([], [], [])
    for prompt in range(PROMPTS):
        queries = prompt_q[prompt].reshape(1, PLEN, KVH, GROUP, HD)
        keys_in = prompt_kv[0, prompt].reshape(1, PLEN, KVH, HD)
        values_in = prompt_kv[1, prompt].reshape(1, PLEN, KVH, HD)
        cotangent = prompt_grad[prompt].reshape(1, PLEN, KVH, GROUP, HD)
        output, dquery, dkeys, dvalues = attend(queries, keys_in, values_in, cotangent, causal)
        out_list.append(output.reshape(PLEN, KVH, GROUP * HD))
        dq_list.append(dquery.astype(jnp.bfloat16).reshape(PLEN, KVH, GROUP * HD))
        grad_list.append(jnp.stack([dkeys[0], dvalues[0]]))
    prompt_grads = jnp.stack(grad_list)
    slot_count = N_PROMPT * N_RESP * N_RESP
    flat_q = resp_q.reshape(slot_count, RLEN, KVH, GROUP, HD)
    flat_kv = jnp.moveaxis(resp_kv.reshape(2, slot_count, RLEN, KVH, HD), 1, 0)
    flat_grad = resp_grad.reshape(slot_count, RLEN, KVH, GROUP, HD)
    flat_owner = resp_prompt.reshape(slot_count).astype(jnp.int32)
    steps_own = jnp.arange(RLEN)
    allowed = jnp.concatenate([jnp.ones((RLEN, PLEN), bool), steps_own[None, :] <= steps_own[:, None]], axis=1)

    def one_slot(totals, record):
        queries, pair, cotangent, owner = record
        source = lax.dynamic_index_in_dim(prompt_kv, owner, 1, keepdims=False)
        keys_in = jnp.concatenate([source[0].reshape(PLEN, KVH, HD), pair[0]], axis=0)[None]
        values_in = jnp.concatenate([source[1].reshape(PLEN, KVH, HD), pair[1]], axis=0)[None]
        output, dquery, dkeys, dvalues = attend(queries[None], keys_in, values_in, cotangent[None], allowed)
        term = jnp.stack([dkeys[0, :PLEN], dvalues[0, :PLEN]])
        totals = totals.at[owner].add(term)
        own_grads = jnp.stack([dkeys[0, PLEN:], dvalues[0, PLEN:]]).astype(jnp.bfloat16)
        return (totals, (output[0], dquery[0].astype(jnp.bfloat16), own_grads))
    totals, (resp_output, resp_dquery, resp_grads) = lax.scan(one_slot, prompt_grads, (flat_q, flat_kv, flat_grad, flat_owner))
    prompt_out = jnp.stack(out_list)
    prompt_dq = jnp.stack(dq_list)
    prompt_dkv = jnp.moveaxis(totals, 1, 0).reshape(2, PROMPTS, PLEN, KVH * HD).astype(jnp.bfloat16)
    resp_out = resp_output.reshape(N_PROMPT, N_RESP, N_RESP, RLEN, KVH, GROUP * HD)
    resp_dq = resp_dquery.reshape(N_PROMPT, N_RESP, N_RESP, RLEN, KVH, GROUP * HD)
    resp_dkv = jnp.moveaxis(resp_grads, 1, 0).reshape(2, N_PROMPT, N_RESP, N_RESP, RLEN, KVH * HD)
    return (prompt_out, prompt_dq, prompt_dkv, resp_out, resp_dq, resp_dkv)
```

```python
import math

import jax
import jax.numpy as jnp
from jax import lax
from jax.sharding import PartitionSpec as P

HD = 128


def attend_blocks(queries, keys_in, values_in, own_keys, own_values, cotangent, shared_ok, own_ok):
    scale = 1.0 / math.sqrt(HD)
    f32 = jnp.float32
    s_sh = jnp.einsum("brkgd,nkd->bkgrn", queries, keys_in, preferred_element_type=f32) * scale
    s_own = jnp.einsum("brkgd,bukd->bkgru", queries, own_keys, preferred_element_type=f32) * scale
    s_sh = jnp.where(shared_ok[:, None, None], s_sh, -1e30)
    s_own = jnp.where(own_ok[:, None, None], s_own, -1e30)
    row_max = jnp.maximum(
        jnp.max(s_sh, axis=-1, keepdims=True), jnp.max(s_own, axis=-1, keepdims=True)
    )
    totals = jnp.sum(jnp.exp(s_sh - row_max), axis=-1, keepdims=True) + jnp.sum(
        jnp.exp(s_own - row_max), axis=-1, keepdims=True
    )
    log_total = row_max + jnp.log(totals)
    p_sh = jnp.exp(s_sh - log_total)
    p_own = jnp.exp(s_own - log_total)
    w_sh = p_sh.astype(jnp.bfloat16)
    w_own = p_own.astype(jnp.bfloat16)
    output = (
        jnp.einsum("bkgrn,nkd->brkgd", w_sh, values_in, preferred_element_type=f32)
        + jnp.einsum("bkgru,bukd->brkgd", w_own, own_values, preferred_element_type=f32)
    ).astype(jnp.bfloat16)
    row_delta = jnp.einsum("brkgd,brkgd->bkgr", cotangent, output, preferred_element_type=f32)
    dp_sh = jnp.einsum("brkgd,nkd->bkgrn", cotangent, values_in, preferred_element_type=f32)
    dp_own = jnp.einsum("brkgd,bukd->bkgru", cotangent, own_values, preferred_element_type=f32)
    ds_sh = (p_sh * (dp_sh - row_delta[..., None])).astype(jnp.bfloat16)
    ds_own = (p_own * (dp_own - row_delta[..., None])).astype(jnp.bfloat16)
    dquery = (
        jnp.einsum("bkgrn,nkd->brkgd", ds_sh, keys_in, preferred_element_type=f32)
        + jnp.einsum("bkgru,bukd->brkgd", ds_own, own_keys, preferred_element_type=f32)
    ) * scale
    dk_sh = jnp.einsum("bkgrn,brkgd->nkd", ds_sh, queries, preferred_element_type=f32) * scale
    dv_sh = jnp.einsum("bkgrn,brkgd->nkd", w_sh, cotangent, preferred_element_type=f32)
    dk_own = jnp.einsum("bkgru,brkgd->bukd", ds_own, queries, preferred_element_type=f32) * scale
    dv_own = jnp.einsum("bkgru,brkgd->bukd", w_own, cotangent, preferred_element_type=f32)
    return output, dquery, dk_sh, dv_sh, dk_own, dv_own


def body(prompt_q, prompt_kv, prompt_grad, resp_q, resp_kv, resp_grad, resp_prompt):
    head_size = HD
    block_rows = prompt_q.shape[1]
    kv_heads = prompt_q.shape[2]
    local_width = prompt_q.shape[3]
    local_heads = local_width // head_size
    full_len = block_rows * lax.axis_size("prompt")
    resp_len = resp_q.shape[3]
    peers = lax.axis_size("resp")
    kv_width = kv_heads * head_size
    gathered = lax.all_gather(prompt_kv, "prompt", axis=2, tiled=True)
    prompt_keys = gathered[0, 0].reshape(full_len, kv_heads, head_size)
    prompt_values = gathered[1, 0].reshape(full_len, kv_heads, head_size)

    order = resp_prompt[0, 0]
    picker = (jnp.arange(peers)[:, None] == order[None, :]).astype(jnp.bfloat16)
    send_q = jnp.einsum(
        "dj,jrkh->drkh", picker, resp_q[0, 0], preferred_element_type=jnp.float32
    ).astype(jnp.bfloat16)
    send_kv = jnp.einsum(
        "dj,cjrh->dcrh", picker, resp_kv[:, 0, 0], preferred_element_type=jnp.float32
    ).astype(jnp.bfloat16)
    send_grad = jnp.einsum(
        "dj,jrkh->drkh", picker, resp_grad[0, 0], preferred_element_type=jnp.float32
    ).astype(jnp.bfloat16)
    got_q, got_kv, got_grad = (
        lax.all_to_all(send_q, "resp", split_axis=0, concat_axis=0, tiled=True),
        lax.all_to_all(send_kv, "resp", split_axis=0, concat_axis=0, tiled=True),
        lax.all_to_all(send_grad, "resp", split_axis=0, concat_axis=0, tiled=True),
    )

    q_shape = (peers + 1, resp_len, kv_heads, local_heads, head_size)
    queries = jnp.concatenate([got_q, prompt_q], axis=0).reshape(q_shape)
    cotangent = jnp.concatenate([got_grad, prompt_grad], axis=0).reshape(q_shape)
    own_kv = jnp.concatenate(
        [got_kv, jnp.zeros((1,) + got_kv.shape[1:], got_kv.dtype)], axis=0
    ).reshape(peers + 1, 2, resp_len, kv_heads, head_size)
    query_rows = lax.axis_index("prompt") * block_rows + jnp.arange(block_rows)
    key_cols = jnp.arange(full_len)
    causal = key_cols[None, :] <= query_rows[:, None]
    shared_ok = jnp.concatenate(
        [jnp.ones((peers, resp_len, full_len), bool), causal[None]], axis=0
    )
    steps_own = jnp.arange(resp_len)
    own_causal = steps_own[None, :] <= steps_own[:, None]
    own_ok = jnp.concatenate(
        [
            jnp.broadcast_to(own_causal, (peers, resp_len, resp_len)),
            jnp.zeros((1, resp_len, resp_len), bool),
        ],
        axis=0,
    )
    out, dq, dk_sh, dv_sh, dk_own, dv_own = attend_blocks(
        queries,
        prompt_keys,
        prompt_values,
        own_kv[:, 0],
        own_kv[:, 1],
        cotangent,
        shared_ok,
        own_ok,
    )
    out = out.reshape(peers + 1, resp_len, kv_heads, local_width)
    dq = dq.astype(jnp.bfloat16).reshape(peers + 1, resp_len, kv_heads, local_width)

    prompt_part = jnp.stack([dk_sh, dv_sh]).reshape(2, full_len, kv_width)
    head_sum = lax.psum_scatter(prompt_part, "head", scatter_dimension=2, tiled=True)
    block_sum = lax.psum_scatter(head_sum, "prompt", scatter_dimension=1, tiled=True)
    own_part = jnp.stack([dk_own[:peers], dv_own[:peers]], axis=1).reshape(
        peers, 2, resp_len, kv_width
    )
    own_sum = lax.psum_scatter(own_part, "head", scatter_dimension=3, tiled=True)
    prompt_dkv = block_sum.astype(jnp.bfloat16)[:, None]
    back_kv = own_sum.astype(jnp.bfloat16)
    ret_out, ret_dq, ret_kv = (
        lax.all_to_all(out[:peers], "resp", split_axis=0, concat_axis=0, tiled=True),
        lax.all_to_all(dq[:peers], "resp", split_axis=0, concat_axis=0, tiled=True),
        lax.all_to_all(back_kv, "resp", split_axis=0, concat_axis=0, tiled=True),
    )
    resp_out = jnp.einsum(
        "dj,drkh->jrkh", picker, ret_out, preferred_element_type=jnp.float32
    ).astype(jnp.bfloat16)[None, None]
    resp_dq = jnp.einsum(
        "dj,drkh->jrkh", picker, ret_dq, preferred_element_type=jnp.float32
    ).astype(jnp.bfloat16)[None, None]
    resp_dkv = jnp.einsum(
        "dj,dcrh->cjrh", picker, ret_kv, preferred_element_type=jnp.float32
    ).astype(jnp.bfloat16)[:, None, None]
    prompt_out = out[peers:]
    prompt_dq = dq[peers:]
    return (prompt_out, prompt_dq, prompt_dkv, resp_out, resp_dq, resp_dkv)


def solution(mesh):
    return jax.shard_map(
        body,
        mesh=mesh,
        in_specs=(
            P("resp", "prompt", None, "head"),
            P(None, "resp", "prompt", None),
            P("resp", "prompt", None, "head"),
            P("prompt", "resp", None, None, None, "head"),
            P(None, "prompt", "resp", None, None, None),
            P("prompt", "resp", None, None, None, "head"),
            P("prompt", "resp", None),
        ),
        out_specs=(
            P("resp", "prompt", None, "head"),
            P("resp", "prompt", None, "head"),
            P(None, "resp", "prompt", "head"),
            P("prompt", "resp", None, None, None, "head"),
            P("prompt", "resp", None, None, None, "head"),
            P(None, "prompt", "resp", None, None, "head"),
        ),
        check_vma=False,
    )
```

```python
import math

import jax
import jax.numpy as jnp
from jax import lax
from jax.sharding import PartitionSpec as P

HD = 128


def attend_blocks(queries, keys_in, values_in, own_keys, own_values, cotangent, shared_ok, own_ok):
    scale = 1.0 / math.sqrt(HD)
    f32 = jnp.float32
    s_sh = jnp.einsum("brkgd,nkd->bkgrn", queries, keys_in, preferred_element_type=f32) * scale
    s_own = jnp.einsum("brkgd,bukd->bkgru", queries, own_keys, preferred_element_type=f32) * scale
    s_sh = jnp.where(shared_ok[:, None, None], s_sh, -1e30)
    s_own = jnp.where(own_ok[:, None, None], s_own, -1e30)
    row_max = jnp.maximum(
        jnp.max(s_sh, axis=-1, keepdims=True), jnp.max(s_own, axis=-1, keepdims=True)
    )
    totals = jnp.sum(jnp.exp(s_sh - row_max), axis=-1, keepdims=True) + jnp.sum(
        jnp.exp(s_own - row_max), axis=-1, keepdims=True
    )
    log_total = row_max + jnp.log(totals)
    p_sh = jnp.exp(s_sh - log_total)
    p_own = jnp.exp(s_own - log_total)
    w_sh = p_sh.astype(jnp.bfloat16)
    w_own = p_own.astype(jnp.bfloat16)
    output = (
        jnp.einsum("bkgrn,nkd->brkgd", w_sh, values_in, preferred_element_type=f32)
        + jnp.einsum("bkgru,bukd->brkgd", w_own, own_values, preferred_element_type=f32)
    ).astype(jnp.bfloat16)
    row_delta = jnp.einsum("brkgd,brkgd->bkgr", cotangent, output, preferred_element_type=f32)
    dp_sh = jnp.einsum("brkgd,nkd->bkgrn", cotangent, values_in, preferred_element_type=f32)
    dp_own = jnp.einsum("brkgd,bukd->bkgru", cotangent, own_values, preferred_element_type=f32)
    ds_sh = (p_sh * (dp_sh - row_delta[..., None])).astype(jnp.bfloat16)
    ds_own = (p_own * (dp_own - row_delta[..., None])).astype(jnp.bfloat16)
    dquery = (
        jnp.einsum("bkgrn,nkd->brkgd", ds_sh, keys_in, preferred_element_type=f32)
        + jnp.einsum("bkgru,bukd->brkgd", ds_own, own_keys, preferred_element_type=f32)
    ) * scale
    dk_sh = jnp.einsum("bkgrn,brkgd->nkd", ds_sh, queries, preferred_element_type=f32) * scale
    dv_sh = jnp.einsum("bkgrn,brkgd->nkd", w_sh, cotangent, preferred_element_type=f32)
    dk_own = jnp.einsum("bkgru,brkgd->bukd", ds_own, queries, preferred_element_type=f32) * scale
    dv_own = jnp.einsum("bkgru,brkgd->bukd", w_own, cotangent, preferred_element_type=f32)
    return output, dquery, dk_sh, dv_sh, dk_own, dv_own


def scatter_sum(x, axis_name, dim):
    n = lax.axis_size(axis_name)
    got = lax.all_to_all(x, axis_name, split_axis=dim, concat_axis=dim, tiled=True)
    shape = x.shape[:dim] + (n, x.shape[dim] // n) + x.shape[dim + 1 :]
    return jnp.sum(got.reshape(shape), axis=dim)


def body(prompt_q, prompt_kv, prompt_grad, resp_q, resp_kv, resp_grad, resp_prompt):
    head_size = HD
    block_rows = prompt_q.shape[1]
    kv_heads = prompt_q.shape[2]
    local_width = prompt_q.shape[3]
    local_heads = local_width // head_size
    full_len = block_rows * lax.axis_size("prompt")
    resp_len = resp_q.shape[3]
    peers = lax.axis_size("resp")
    kv_width = kv_heads * head_size
    gathered = lax.all_gather(prompt_kv, "prompt", axis=2, tiled=True)
    prompt_keys = gathered[0, 0].reshape(full_len, kv_heads, head_size)
    prompt_values = gathered[1, 0].reshape(full_len, kv_heads, head_size)

    order = resp_prompt[0, 0]
    picker = (jnp.arange(peers)[:, None] == order[None, :]).astype(jnp.bfloat16)
    send_q = jnp.einsum(
        "dj,jrkh->drkh", picker, resp_q[0, 0], preferred_element_type=jnp.float32
    ).astype(jnp.bfloat16)
    send_kv = jnp.einsum(
        "dj,cjrh->dcrh", picker, resp_kv[:, 0, 0], preferred_element_type=jnp.float32
    ).astype(jnp.bfloat16)
    send_grad = jnp.einsum(
        "dj,jrkh->drkh", picker, resp_grad[0, 0], preferred_element_type=jnp.float32
    ).astype(jnp.bfloat16)
    got_q, got_kv, got_grad = (
        lax.all_to_all(send_q, "resp", split_axis=0, concat_axis=0, tiled=True),
        lax.all_to_all(send_kv, "resp", split_axis=0, concat_axis=0, tiled=True),
        lax.all_to_all(send_grad, "resp", split_axis=0, concat_axis=0, tiled=True),
    )

    q_shape = (peers + 1, resp_len, kv_heads, local_heads, head_size)
    queries = jnp.concatenate([got_q, prompt_q], axis=0).reshape(q_shape)
    cotangent = jnp.concatenate([got_grad, prompt_grad], axis=0).reshape(q_shape)
    own_kv = jnp.concatenate(
        [got_kv, jnp.zeros((1,) + got_kv.shape[1:], got_kv.dtype)], axis=0
    ).reshape(peers + 1, 2, resp_len, kv_heads, head_size)
    query_rows = lax.axis_index("prompt") * block_rows + jnp.arange(block_rows)
    key_cols = jnp.arange(full_len)
    causal = key_cols[None, :] <= query_rows[:, None]
    shared_ok = jnp.concatenate(
        [jnp.ones((peers, resp_len, full_len), bool), causal[None]], axis=0
    )
    steps_own = jnp.arange(resp_len)
    own_causal = steps_own[None, :] <= steps_own[:, None]
    own_ok = jnp.concatenate(
        [
            jnp.broadcast_to(own_causal, (peers, resp_len, resp_len)),
            jnp.zeros((1, resp_len, resp_len), bool),
        ],
        axis=0,
    )
    out, dq, dk_sh, dv_sh, dk_own, dv_own = attend_blocks(
        queries,
        prompt_keys,
        prompt_values,
        own_kv[:, 0],
        own_kv[:, 1],
        cotangent,
        shared_ok,
        own_ok,
    )
    out = out.reshape(peers + 1, resp_len, kv_heads, local_width)
    dq = dq.astype(jnp.bfloat16).reshape(peers + 1, resp_len, kv_heads, local_width)

    prompt_part = jnp.stack([dk_sh, dv_sh]).reshape(2, full_len, kv_width)
    head_sum = scatter_sum(prompt_part, "head", 2)
    block_sum = scatter_sum(head_sum, "prompt", 1)
    own_part = jnp.stack([dk_own[:peers], dv_own[:peers]], axis=1).reshape(
        peers, 2, resp_len, kv_width
    )
    own_sum = scatter_sum(own_part, "head", 3)
    prompt_dkv = block_sum.astype(jnp.bfloat16)[:, None]
    back_kv = own_sum.astype(jnp.bfloat16)
    ret_out, ret_dq, ret_kv = (
        lax.all_to_all(out[:peers], "resp", split_axis=0, concat_axis=0, tiled=True),
        lax.all_to_all(dq[:peers], "resp", split_axis=0, concat_axis=0, tiled=True),
        lax.all_to_all(back_kv, "resp", split_axis=0, concat_axis=0, tiled=True),
    )
    resp_out = jnp.einsum(
        "dj,drkh->jrkh", picker, ret_out, preferred_element_type=jnp.float32
    ).astype(jnp.bfloat16)[None, None]
    resp_dq = jnp.einsum(
        "dj,drkh->jrkh", picker, ret_dq, preferred_element_type=jnp.float32
    ).astype(jnp.bfloat16)[None, None]
    resp_dkv = jnp.einsum(
        "dj,dcrh->cjrh", picker, ret_kv, preferred_element_type=jnp.float32
    ).astype(jnp.bfloat16)[:, None, None]
    prompt_out = out[peers:]
    prompt_dq = dq[peers:]
    return (prompt_out, prompt_dq, prompt_dkv, resp_out, resp_dq, resp_dkv)


def solution(mesh):
    return jax.shard_map(
        body,
        mesh=mesh,
        in_specs=(
            P("resp", "prompt", None, "head"),
            P(None, "resp", "prompt", None),
            P("resp", "prompt", None, "head"),
            P("prompt", "resp", None, None, None, "head"),
            P(None, "prompt", "resp", None, None, None),
            P("prompt", "resp", None, None, None, "head"),
            P("prompt", "resp", None),
        ),
        out_specs=(
            P("resp", "prompt", None, "head"),
            P("resp", "prompt", None, "head"),
            P(None, "resp", "prompt", "head"),
            P("prompt", "resp", None, None, None, "head"),
            P("prompt", "resp", None, None, None, "head"),
            P(None, "prompt", "resp", None, None, "head"),
        ),
        check_vma=False,
    )
```

```python
import math

import jax
import jax.numpy as jnp
from jax import lax
from jax.sharding import PartitionSpec as P

HD = 128


def attend_blocks(queries, keys_in, values_in, own_keys, own_values, cotangent, shared_ok, own_ok):
    scale = 1.0 / math.sqrt(HD)
    f32 = jnp.float32
    s_sh = jnp.einsum("brkgd,nkd->bkgrn", queries, keys_in, preferred_element_type=f32) * scale
    s_own = jnp.einsum("brkgd,bukd->bkgru", queries, own_keys, preferred_element_type=f32) * scale
    s_sh = jnp.where(shared_ok[:, None, None], s_sh, -1e30)
    s_own = jnp.where(own_ok[:, None, None], s_own, -1e30)
    row_max = jnp.maximum(
        jnp.max(s_sh, axis=-1, keepdims=True), jnp.max(s_own, axis=-1, keepdims=True)
    )
    totals = jnp.sum(jnp.exp(s_sh - row_max), axis=-1, keepdims=True) + jnp.sum(
        jnp.exp(s_own - row_max), axis=-1, keepdims=True
    )
    log_total = row_max + jnp.log(totals)
    p_sh = jnp.exp(s_sh - log_total)
    p_own = jnp.exp(s_own - log_total)
    w_sh = p_sh.astype(jnp.bfloat16)
    w_own = p_own.astype(jnp.bfloat16)
    output = (
        jnp.einsum("bkgrn,nkd->brkgd", w_sh, values_in, preferred_element_type=f32)
        + jnp.einsum("bkgru,bukd->brkgd", w_own, own_values, preferred_element_type=f32)
    ).astype(jnp.bfloat16)
    row_delta = jnp.einsum("brkgd,brkgd->bkgr", cotangent, output, preferred_element_type=f32)
    dp_sh = jnp.einsum("brkgd,nkd->bkgrn", cotangent, values_in, preferred_element_type=f32)
    dp_own = jnp.einsum("brkgd,bukd->bkgru", cotangent, own_values, preferred_element_type=f32)
    ds_sh = (p_sh * (dp_sh - row_delta[..., None])).astype(jnp.bfloat16)
    ds_own = (p_own * (dp_own - row_delta[..., None])).astype(jnp.bfloat16)
    dquery = (
        jnp.einsum("bkgrn,nkd->brkgd", ds_sh, keys_in, preferred_element_type=f32)
        + jnp.einsum("bkgru,bukd->brkgd", ds_own, own_keys, preferred_element_type=f32)
    ) * scale
    dk_sh = jnp.einsum("bkgrn,brkgd->nkd", ds_sh, queries, preferred_element_type=f32) * scale
    dv_sh = jnp.einsum("bkgrn,brkgd->nkd", w_sh, cotangent, preferred_element_type=f32)
    dk_own = jnp.einsum("bkgru,brkgd->bukd", ds_own, queries, preferred_element_type=f32) * scale
    dv_own = jnp.einsum("bkgru,brkgd->bukd", w_own, cotangent, preferred_element_type=f32)
    return output, dquery, dk_sh, dv_sh, dk_own, dv_own


def scatter_sum(x, axis_name, dim):
    n = lax.axis_size(axis_name)
    got = lax.all_to_all(x, axis_name, split_axis=dim, concat_axis=dim, tiled=True)
    shape = x.shape[:dim] + (n, x.shape[dim] // n) + x.shape[dim + 1 :]
    return jnp.sum(got.reshape(shape), axis=dim)


def body(prompt_q, prompt_kv, prompt_grad, resp_q, resp_kv, resp_grad, resp_prompt):
    head_size = HD
    block_rows = prompt_q.shape[1]
    kv_heads = prompt_q.shape[2]
    local_width = prompt_q.shape[3]
    local_heads = local_width // head_size
    full_len = block_rows * lax.axis_size("prompt")
    resp_len = resp_q.shape[3]
    peers = lax.axis_size("resp")
    kv_width = kv_heads * head_size
    q_width = kv_heads * local_width
    gathered = lax.all_gather(prompt_kv, "prompt", axis=2, tiled=True)
    prompt_keys = gathered[0, 0].reshape(full_len, kv_heads, head_size)
    prompt_values = gathered[1, 0].reshape(full_len, kv_heads, head_size)

    order = resp_prompt[0, 0]
    picker = (jnp.arange(peers)[:, None] == order[None, :]).astype(jnp.bfloat16)
    stacked = jnp.concatenate(
        [
            resp_q[0, 0].reshape(peers, resp_len, q_width),
            jnp.moveaxis(resp_kv[:, 0, 0], 0, 2).reshape(peers, resp_len, 2 * kv_width),
            resp_grad[0, 0].reshape(peers, resp_len, q_width),
        ],
        axis=-1,
    )
    send = jnp.einsum(
        "dj,jrh->drh", picker, stacked, preferred_element_type=jnp.float32
    ).astype(jnp.bfloat16)
    got = lax.all_to_all(send, "resp", split_axis=0, concat_axis=0, tiled=True)
    got_q = got[..., :q_width]
    got_kv = jnp.moveaxis(
        got[..., q_width : q_width + 2 * kv_width].reshape(peers, resp_len, 2, kv_width), 2, 1
    )
    got_grad = got[..., q_width + 2 * kv_width :]

    q_shape = (peers + 1, resp_len, kv_heads, local_heads, head_size)
    queries = jnp.concatenate([got_q, prompt_q[0].reshape(1, resp_len, q_width)], axis=0).reshape(q_shape)
    cotangent = jnp.concatenate([got_grad, prompt_grad[0].reshape(1, resp_len, q_width)], axis=0).reshape(q_shape)
    own_kv = jnp.concatenate(
        [got_kv, jnp.zeros((1,) + got_kv.shape[1:], got_kv.dtype)], axis=0
    ).reshape(peers + 1, 2, resp_len, kv_heads, head_size)
    query_rows = lax.axis_index("prompt") * block_rows + jnp.arange(block_rows)
    key_cols = jnp.arange(full_len)
    causal = key_cols[None, :] <= query_rows[:, None]
    shared_ok = jnp.concatenate(
        [jnp.ones((peers, resp_len, full_len), bool), causal[None]], axis=0
    )
    steps_own = jnp.arange(resp_len)
    own_causal = steps_own[None, :] <= steps_own[:, None]
    own_ok = jnp.concatenate(
        [
            jnp.broadcast_to(own_causal, (peers, resp_len, resp_len)),
            jnp.zeros((1, resp_len, resp_len), bool),
        ],
        axis=0,
    )
    out, dq, dk_sh, dv_sh, dk_own, dv_own = attend_blocks(
        queries,
        prompt_keys,
        prompt_values,
        own_kv[:, 0],
        own_kv[:, 1],
        cotangent,
        shared_ok,
        own_ok,
    )
    out = out.reshape(peers + 1, resp_len, kv_heads, local_width)
    dq = dq.astype(jnp.bfloat16).reshape(peers + 1, resp_len, kv_heads, local_width)

    prompt_part = jnp.stack([dk_sh, dv_sh]).reshape(2, full_len, kv_width)
    head_sum = scatter_sum(prompt_part, "head", 2)
    block_sum = scatter_sum(head_sum, "prompt", 1)
    own_part = jnp.stack([dk_own[:peers], dv_own[:peers]], axis=1).reshape(
        peers, 2, resp_len, kv_width
    )
    own_sum = scatter_sum(own_part, "head", 3)
    prompt_dkv = block_sum.astype(jnp.bfloat16)[:, None]
    back_kv = own_sum.astype(jnp.bfloat16)
    back = jnp.concatenate(
        [
            out[:peers].reshape(peers, resp_len, q_width),
            dq[:peers].reshape(peers, resp_len, q_width),
            jnp.moveaxis(back_kv, 1, 2).reshape(peers, resp_len, kv_width),
        ],
        axis=-1,
    )
    ret = lax.all_to_all(back, "resp", split_axis=0, concat_axis=0, tiled=True)
    mine = jnp.einsum(
        "dj,drh->jrh", picker, ret, preferred_element_type=jnp.float32
    ).astype(jnp.bfloat16)
    resp_out = mine[..., :q_width].reshape(peers, resp_len, kv_heads, local_width)[None, None]
    resp_dq = mine[..., q_width : 2 * q_width].reshape(
        peers, resp_len, kv_heads, local_width
    )[None, None]
    resp_dkv = jnp.moveaxis(
        mine[..., 2 * q_width :].reshape(peers, resp_len, 2, kv_width // 2), 2, 0
    )[:, None, None]
    prompt_out = out[peers:]
    prompt_dq = dq[peers:]
    return (prompt_out, prompt_dq, prompt_dkv, resp_out, resp_dq, resp_dkv)


def solution(mesh):
    return jax.shard_map(
        body,
        mesh=mesh,
        in_specs=(
            P("resp", "prompt", None, "head"),
            P(None, "resp", "prompt", None),
            P("resp", "prompt", None, "head"),
            P("prompt", "resp", None, None, None, "head"),
            P(None, "prompt", "resp", None, None, None),
            P("prompt", "resp", None, None, None, "head"),
            P("prompt", "resp", None),
        ),
        out_specs=(
            P("resp", "prompt", None, "head"),
            P("resp", "prompt", None, "head"),
            P(None, "resp", "prompt", "head"),
            P("prompt", "resp", None, None, None, "head"),
            P("prompt", "resp", None, None, None, "head"),
            P(None, "prompt", "resp", None, None, "head"),
        ),
        check_vma=False,
    )
```

```python
import math

import jax
import jax.numpy as jnp
from jax import lax
from jax.sharding import PartitionSpec as P

HD = 128


def attend_blocks(queries, keys_in, values_in, own_keys, own_values, cotangent, shared_ok, own_ok):
    scale = 1.0 / math.sqrt(HD)
    f32 = jnp.float32
    s_sh = jnp.einsum("brkgd,nkd->bkgrn", queries, keys_in, preferred_element_type=f32) * scale
    s_own = jnp.einsum("brkgd,bukd->bkgru", queries, own_keys, preferred_element_type=f32) * scale
    s_sh = jnp.where(shared_ok[:, None, None], s_sh, -1e30)
    s_own = jnp.where(own_ok[:, None, None], s_own, -1e30)
    row_max = jnp.maximum(
        jnp.max(s_sh, axis=-1, keepdims=True), jnp.max(s_own, axis=-1, keepdims=True)
    )
    totals = jnp.sum(jnp.exp(s_sh - row_max), axis=-1, keepdims=True) + jnp.sum(
        jnp.exp(s_own - row_max), axis=-1, keepdims=True
    )
    log_total = row_max + jnp.log(totals)
    p_sh = jnp.exp(s_sh - log_total)
    p_own = jnp.exp(s_own - log_total)
    w_sh = p_sh.astype(jnp.bfloat16)
    w_own = p_own.astype(jnp.bfloat16)
    output = (
        jnp.einsum("bkgrn,nkd->brkgd", w_sh, values_in, preferred_element_type=f32)
        + jnp.einsum("bkgru,bukd->brkgd", w_own, own_values, preferred_element_type=f32)
    ).astype(jnp.bfloat16)
    row_delta = jnp.einsum("brkgd,brkgd->bkgr", cotangent, output, preferred_element_type=f32)
    dp_sh = jnp.einsum("brkgd,nkd->bkgrn", cotangent, values_in, preferred_element_type=f32)
    dp_own = jnp.einsum("brkgd,bukd->bkgru", cotangent, own_values, preferred_element_type=f32)
    ds_sh = (p_sh * (dp_sh - row_delta[..., None])).astype(jnp.bfloat16)
    ds_own = (p_own * (dp_own - row_delta[..., None])).astype(jnp.bfloat16)
    dquery = (
        jnp.einsum("bkgrn,nkd->brkgd", ds_sh, keys_in, preferred_element_type=f32)
        + jnp.einsum("bkgru,bukd->brkgd", ds_own, own_keys, preferred_element_type=f32)
    ) * scale
    dk_sh = jnp.einsum("bkgrn,brkgd->nkd", ds_sh, queries, preferred_element_type=f32) * scale
    dv_sh = jnp.einsum("bkgrn,brkgd->nkd", w_sh, cotangent, preferred_element_type=f32)
    dk_own = jnp.einsum("bkgru,brkgd->bukd", ds_own, queries, preferred_element_type=f32) * scale
    dv_own = jnp.einsum("bkgru,brkgd->bukd", w_own, cotangent, preferred_element_type=f32)
    return output, dquery, dk_sh, dv_sh, dk_own, dv_own


def scatter_sum(x, axis_name, dim):
    n = lax.axis_size(axis_name)
    got = lax.all_to_all(x, axis_name, split_axis=dim, concat_axis=dim, tiled=True)
    shape = x.shape[:dim] + (n, x.shape[dim] // n) + x.shape[dim + 1 :]
    return jnp.sum(got.reshape(shape), axis=dim)


def body(prompt_q, prompt_kv, prompt_grad, resp_q, resp_kv, resp_grad, resp_prompt):
    head_size = HD
    block_rows = prompt_q.shape[1]
    kv_heads = prompt_q.shape[2]
    local_width = prompt_q.shape[3]
    local_heads = local_width // head_size
    full_len = block_rows * lax.axis_size("prompt")
    resp_len = resp_q.shape[3]
    peers = lax.axis_size("resp")
    kv_width = kv_heads * head_size
    q_width = kv_heads * local_width
    blocks = lax.axis_size("prompt")
    repeated = jnp.broadcast_to(prompt_kv[:, 0][:, None], (2, blocks) + prompt_kv.shape[2:])
    gathered = lax.all_to_all(repeated, "prompt", split_axis=1, concat_axis=1, tiled=True)
    prompt_keys = gathered[0].reshape(full_len, kv_heads, head_size)
    prompt_values = gathered[1].reshape(full_len, kv_heads, head_size)

    order = resp_prompt[0, 0]
    picker = (jnp.arange(peers)[:, None] == order[None, :]).astype(jnp.bfloat16)
    stacked = jnp.concatenate(
        [
            resp_q[0, 0].reshape(peers, resp_len, q_width),
            jnp.moveaxis(resp_kv[:, 0, 0], 0, 2).reshape(peers, resp_len, 2 * kv_width),
            resp_grad[0, 0].reshape(peers, resp_len, q_width),
        ],
        axis=-1,
    )
    send = jnp.einsum(
        "dj,jrh->drh", picker, stacked, preferred_element_type=jnp.float32
    ).astype(jnp.bfloat16)
    got = lax.all_to_all(send, "resp", split_axis=0, concat_axis=0, tiled=True)
    got_q = got[..., :q_width]
    got_kv = jnp.moveaxis(
        got[..., q_width : q_width + 2 * kv_width].reshape(peers, resp_len, 2, kv_width), 2, 1
    )
    got_grad = got[..., q_width + 2 * kv_width :]

    q_shape = (peers + 1, resp_len, kv_heads, local_heads, head_size)
    queries = jnp.concatenate([got_q, prompt_q[0].reshape(1, resp_len, q_width)], axis=0).reshape(q_shape)
    cotangent = jnp.concatenate([got_grad, prompt_grad[0].reshape(1, resp_len, q_width)], axis=0).reshape(q_shape)
    own_kv = jnp.concatenate(
        [got_kv, jnp.zeros((1,) + got_kv.shape[1:], got_kv.dtype)], axis=0
    ).reshape(peers + 1, 2, resp_len, kv_heads, head_size)
    query_rows = lax.axis_index("prompt") * block_rows + jnp.arange(block_rows)
    key_cols = jnp.arange(full_len)
    causal = key_cols[None, :] <= query_rows[:, None]
    shared_ok = jnp.concatenate(
        [jnp.ones((peers, resp_len, full_len), bool), causal[None]], axis=0
    )
    steps_own = jnp.arange(resp_len)
    own_causal = steps_own[None, :] <= steps_own[:, None]
    own_ok = jnp.concatenate(
        [
            jnp.broadcast_to(own_causal, (peers, resp_len, resp_len)),
            jnp.zeros((1, resp_len, resp_len), bool),
        ],
        axis=0,
    )
    out, dq, dk_sh, dv_sh, dk_own, dv_own = attend_blocks(
        queries,
        prompt_keys,
        prompt_values,
        own_kv[:, 0],
        own_kv[:, 1],
        cotangent,
        shared_ok,
        own_ok,
    )
    out = out.reshape(peers + 1, resp_len, kv_heads, local_width)
    dq = dq.astype(jnp.bfloat16).reshape(peers + 1, resp_len, kv_heads, local_width)

    prompt_part = jnp.stack([dk_sh, dv_sh]).reshape(2, full_len, kv_width)
    head_sum = scatter_sum(prompt_part, "head", 2)
    block_sum = scatter_sum(head_sum, "prompt", 1)
    own_part = jnp.stack([dk_own[:peers], dv_own[:peers]], axis=1).reshape(
        peers, 2, resp_len, kv_width
    )
    own_sum = scatter_sum(own_part, "head", 3)
    prompt_dkv = block_sum.astype(jnp.bfloat16)[:, None]
    back_kv = own_sum.astype(jnp.bfloat16)
    back = jnp.concatenate(
        [
            out[:peers].reshape(peers, resp_len, q_width),
            dq[:peers].reshape(peers, resp_len, q_width),
            jnp.moveaxis(back_kv, 1, 2).reshape(peers, resp_len, kv_width),
        ],
        axis=-1,
    )
    ret = lax.all_to_all(back, "resp", split_axis=0, concat_axis=0, tiled=True)
    mine = jnp.einsum(
        "dj,drh->jrh", picker, ret, preferred_element_type=jnp.float32
    ).astype(jnp.bfloat16)
    resp_out = mine[..., :q_width].reshape(peers, resp_len, kv_heads, local_width)[None, None]
    resp_dq = mine[..., q_width : 2 * q_width].reshape(
        peers, resp_len, kv_heads, local_width
    )[None, None]
    resp_dkv = jnp.moveaxis(
        mine[..., 2 * q_width :].reshape(peers, resp_len, 2, kv_width // 2), 2, 0
    )[:, None, None]
    prompt_out = out[peers:]
    prompt_dq = dq[peers:]
    return (prompt_out, prompt_dq, prompt_dkv, resp_out, resp_dq, resp_dkv)


def solution(mesh):
    return jax.shard_map(
        body,
        mesh=mesh,
        in_specs=(
            P("resp", "prompt", None, "head"),
            P(None, "resp", "prompt", None),
            P("resp", "prompt", None, "head"),
            P("prompt", "resp", None, None, None, "head"),
            P(None, "prompt", "resp", None, None, None),
            P("prompt", "resp", None, None, None, "head"),
            P("prompt", "resp", None),
        ),
        out_specs=(
            P("resp", "prompt", None, "head"),
            P("resp", "prompt", None, "head"),
            P(None, "resp", "prompt", "head"),
            P("prompt", "resp", None, None, None, "head"),
            P("prompt", "resp", None, None, None, "head"),
            P(None, "prompt", "resp", None, None, "head"),
        ),
        check_vma=False,
    )
```

```python
import math

import jax
import jax.numpy as jnp
from jax import lax
from jax.sharding import PartitionSpec as P

HD = 128


def attend_blocks(queries, keys_in, values_in, own_keys, own_values, cotangent, shared_ok, own_ok):
    scale = 1.0 / math.sqrt(HD)
    f32 = jnp.float32
    s_sh = jnp.einsum("brkgd,nkd->bkgrn", queries, keys_in, preferred_element_type=f32) * scale
    s_own = jnp.einsum("brkgd,bukd->bkgru", queries, own_keys, preferred_element_type=f32) * scale
    s_sh = jnp.where(shared_ok[:, None, None], s_sh, -1e30)
    s_own = jnp.where(own_ok[:, None, None], s_own, -1e30)
    row_max = jnp.maximum(
        jnp.max(s_sh, axis=-1, keepdims=True), jnp.max(s_own, axis=-1, keepdims=True)
    )
    totals = jnp.sum(jnp.exp(s_sh - row_max), axis=-1, keepdims=True) + jnp.sum(
        jnp.exp(s_own - row_max), axis=-1, keepdims=True
    )
    log_total = row_max + jnp.log(totals)
    p_sh = jnp.exp(s_sh - log_total)
    p_own = jnp.exp(s_own - log_total)
    w_sh = p_sh.astype(jnp.bfloat16)
    w_own = p_own.astype(jnp.bfloat16)
    output = (
        jnp.einsum("bkgrn,nkd->brkgd", w_sh, values_in, preferred_element_type=f32)
        + jnp.einsum("bkgru,bukd->brkgd", w_own, own_values, preferred_element_type=f32)
    ).astype(jnp.bfloat16)
    row_delta = jnp.einsum("brkgd,brkgd->bkgr", cotangent, output, preferred_element_type=f32)
    dp_sh = jnp.einsum("brkgd,nkd->bkgrn", cotangent, values_in, preferred_element_type=f32)
    dp_own = jnp.einsum("brkgd,bukd->bkgru", cotangent, own_values, preferred_element_type=f32)
    ds_sh = (p_sh * (dp_sh - row_delta[..., None])).astype(jnp.bfloat16)
    ds_own = (p_own * (dp_own - row_delta[..., None])).astype(jnp.bfloat16)
    dquery = (
        jnp.einsum("bkgrn,nkd->brkgd", ds_sh, keys_in, preferred_element_type=f32)
        + jnp.einsum("bkgru,bukd->brkgd", ds_own, own_keys, preferred_element_type=f32)
    ) * scale
    dk_sh = jnp.einsum("bkgrn,brkgd->nkd", ds_sh, queries, preferred_element_type=f32) * scale
    dv_sh = jnp.einsum("bkgrn,brkgd->nkd", w_sh, cotangent, preferred_element_type=f32)
    dk_own = jnp.einsum("bkgru,brkgd->bukd", ds_own, queries, preferred_element_type=f32) * scale
    dv_own = jnp.einsum("bkgru,brkgd->bukd", w_own, cotangent, preferred_element_type=f32)
    return output, dquery, dk_sh, dv_sh, dk_own, dv_own


def scatter_sum(x, axis_name, dim):
    n = lax.axis_size(axis_name)
    got = lax.all_to_all(x, axis_name, split_axis=dim, concat_axis=dim, tiled=True)
    shape = x.shape[:dim] + (n, x.shape[dim] // n) + x.shape[dim + 1 :]
    return jnp.sum(got.reshape(shape), axis=dim)


def all_gather_by_all_to_all(x, axis_name):
    n = lax.axis_size(axis_name)
    repeated = jnp.broadcast_to(x[None], (n,) + x.shape)
    return lax.all_to_all(repeated, axis_name, split_axis=0, concat_axis=0, tiled=True).reshape(
        (n * x.shape[0],) + x.shape[1:]
    )


def body(prompt_q, prompt_kv, prompt_grad, resp_q, resp_kv, resp_grad, resp_prompt):
    head_size = HD
    block_rows = prompt_q.shape[1]
    kv_heads = prompt_q.shape[2]
    local_width = prompt_q.shape[3]
    local_heads = local_width // head_size
    full_len = block_rows * lax.axis_size("prompt")
    resp_len = resp_q.shape[3]
    peers = lax.axis_size("resp")
    kv_width = kv_heads * head_size
    q_width = kv_heads * local_width
    half = lax.dynamic_index_in_dim(prompt_kv[:, 0], lax.axis_index("head"), 0, keepdims=False)
    gathered_half = all_gather_by_all_to_all(half, "prompt")
    gathered = all_gather_by_all_to_all(gathered_half.reshape(1, full_len, kv_width), "head")
    prompt_keys = gathered[0].reshape(full_len, kv_heads, head_size)
    prompt_values = gathered[1].reshape(full_len, kv_heads, head_size)

    order = resp_prompt[0, 0]
    picker = (jnp.arange(peers)[:, None] == order[None, :]).astype(jnp.bfloat16)
    stacked = jnp.concatenate(
        [
            resp_q[0, 0].reshape(peers, resp_len, q_width),
            jnp.moveaxis(resp_kv[:, 0, 0], 0, 2).reshape(peers, resp_len, 2 * kv_width),
            resp_grad[0, 0].reshape(peers, resp_len, q_width),
        ],
        axis=-1,
    )
    send = jnp.einsum(
        "dj,jrh->drh", picker, stacked, preferred_element_type=jnp.float32
    ).astype(jnp.bfloat16)
    got = lax.all_to_all(send, "resp", split_axis=0, concat_axis=0, tiled=True)
    got_q = got[..., :q_width]
    got_kv = jnp.moveaxis(
        got[..., q_width : q_width + 2 * kv_width].reshape(peers, resp_len, 2, kv_width), 2, 1
    )
    got_grad = got[..., q_width + 2 * kv_width :]

    q_shape = (peers + 1, resp_len, kv_heads, local_heads, head_size)
    queries = jnp.concatenate([got_q, prompt_q[0].reshape(1, resp_len, q_width)], axis=0).reshape(q_shape)
    cotangent = jnp.concatenate([got_grad, prompt_grad[0].reshape(1, resp_len, q_width)], axis=0).reshape(q_shape)
    own_kv = jnp.concatenate(
        [got_kv, jnp.zeros((1,) + got_kv.shape[1:], got_kv.dtype)], axis=0
    ).reshape(peers + 1, 2, resp_len, kv_heads, head_size)
    query_rows = lax.axis_index("prompt") * block_rows + jnp.arange(block_rows)
    key_cols = jnp.arange(full_len)
    causal = key_cols[None, :] <= query_rows[:, None]
    shared_ok = jnp.concatenate(
        [jnp.ones((peers, resp_len, full_len), bool), causal[None]], axis=0
    )
    steps_own = jnp.arange(resp_len)
    own_causal = steps_own[None, :] <= steps_own[:, None]
    own_ok = jnp.concatenate(
        [
            jnp.broadcast_to(own_causal, (peers, resp_len, resp_len)),
            jnp.zeros((1, resp_len, resp_len), bool),
        ],
        axis=0,
    )
    out, dq, dk_sh, dv_sh, dk_own, dv_own = attend_blocks(
        queries,
        prompt_keys,
        prompt_values,
        own_kv[:, 0],
        own_kv[:, 1],
        cotangent,
        shared_ok,
        own_ok,
    )
    out = out.reshape(peers + 1, resp_len, kv_heads, local_width)
    dq = dq.astype(jnp.bfloat16).reshape(peers + 1, resp_len, kv_heads, local_width)

    block_sum = jnp.stack(
        [
            scatter_sum(scatter_sum(part.reshape(full_len, kv_width), "head", 1), "prompt", 0)
            for part in (dk_sh, dv_sh)
        ]
    )
    own_part = jnp.stack([dk_own[:peers], dv_own[:peers]], axis=1).reshape(
        peers, 2, resp_len, kv_width
    )
    own_sum = scatter_sum(own_part, "head", 3)
    prompt_dkv = block_sum.astype(jnp.bfloat16)[:, None]
    back_kv = own_sum.astype(jnp.bfloat16)
    back = jnp.concatenate(
        [
            out[:peers].reshape(peers, resp_len, q_width),
            dq[:peers].reshape(peers, resp_len, q_width),
            jnp.moveaxis(back_kv, 1, 2).reshape(peers, resp_len, kv_width),
        ],
        axis=-1,
    )
    ret = lax.all_to_all(back, "resp", split_axis=0, concat_axis=0, tiled=True)
    mine = jnp.einsum(
        "dj,drh->jrh", picker, ret, preferred_element_type=jnp.float32
    ).astype(jnp.bfloat16)
    resp_out = mine[..., :q_width].reshape(peers, resp_len, kv_heads, local_width)[None, None]
    resp_dq = mine[..., q_width : 2 * q_width].reshape(
        peers, resp_len, kv_heads, local_width
    )[None, None]
    resp_dkv = jnp.moveaxis(
        mine[..., 2 * q_width :].reshape(peers, resp_len, 2, kv_width // 2), 2, 0
    )[:, None, None]
    prompt_out = out[peers:]
    prompt_dq = dq[peers:]
    return (prompt_out, prompt_dq, prompt_dkv, resp_out, resp_dq, resp_dkv)


def solution(mesh):
    return jax.shard_map(
        body,
        mesh=mesh,
        in_specs=(
            P("resp", "prompt", None, "head"),
            P(None, "resp", "prompt", None),
            P("resp", "prompt", None, "head"),
            P("prompt", "resp", None, None, None, "head"),
            P(None, "prompt", "resp", None, None, None),
            P("prompt", "resp", None, None, None, "head"),
            P("prompt", "resp", None),
        ),
        out_specs=(
            P("resp", "prompt", None, "head"),
            P("resp", "prompt", None, "head"),
            P(None, "resp", "prompt", "head"),
            P("prompt", "resp", None, None, None, "head"),
            P("prompt", "resp", None, None, None, "head"),
            P(None, "prompt", "resp", None, None, "head"),
        ),
        check_vma=False,
    )
```

```python
import math

import jax
import jax.numpy as jnp
from jax import lax
from jax.sharding import PartitionSpec as P

HD = 128


def attend_blocks(queries, keys_in, values_in, own_keys, own_values, cotangent, shared_ok, own_ok):
    scale = 1.0 / math.sqrt(HD)
    f32 = jnp.float32
    s_sh = jnp.einsum("brkgd,nkd->bkgrn", queries, keys_in, preferred_element_type=f32) * scale
    s_own = jnp.einsum("brkgd,bukd->bkgru", queries, own_keys, preferred_element_type=f32) * scale
    s_sh = jnp.where(shared_ok[:, None, None], s_sh, -1e30)
    s_own = jnp.where(own_ok[:, None, None], s_own, -1e30)
    row_max = jnp.maximum(
        jnp.max(s_sh, axis=-1, keepdims=True), jnp.max(s_own, axis=-1, keepdims=True)
    )
    totals = jnp.sum(jnp.exp(s_sh - row_max), axis=-1, keepdims=True) + jnp.sum(
        jnp.exp(s_own - row_max), axis=-1, keepdims=True
    )
    log_total = row_max + jnp.log(totals)
    p_sh = jnp.exp(s_sh - log_total)
    p_own = jnp.exp(s_own - log_total)
    w_sh = p_sh.astype(jnp.bfloat16)
    w_own = p_own.astype(jnp.bfloat16)
    output = (
        jnp.einsum("bkgrn,nkd->brkgd", w_sh, values_in, preferred_element_type=f32)
        + jnp.einsum("bkgru,bukd->brkgd", w_own, own_values, preferred_element_type=f32)
    ).astype(jnp.bfloat16)
    row_delta = jnp.einsum("brkgd,brkgd->bkgr", cotangent, output, preferred_element_type=f32)
    dp_sh = jnp.einsum("brkgd,nkd->bkgrn", cotangent, values_in, preferred_element_type=f32)
    dp_own = jnp.einsum("brkgd,bukd->bkgru", cotangent, own_values, preferred_element_type=f32)
    ds_sh = (p_sh * (dp_sh - row_delta[..., None])).astype(jnp.bfloat16)
    ds_own = (p_own * (dp_own - row_delta[..., None])).astype(jnp.bfloat16)
    dquery = (
        jnp.einsum("bkgrn,nkd->brkgd", ds_sh, keys_in, preferred_element_type=f32)
        + jnp.einsum("bkgru,bukd->brkgd", ds_own, own_keys, preferred_element_type=f32)
    ) * scale
    dk_sh = jnp.einsum("bkgrn,brkgd->nkd", ds_sh, queries, preferred_element_type=f32) * scale
    dv_sh = jnp.einsum("bkgrn,brkgd->nkd", w_sh, cotangent, preferred_element_type=f32)
    dk_own = jnp.einsum("bkgru,brkgd->bukd", ds_own, queries, preferred_element_type=f32) * scale
    dv_own = jnp.einsum("bkgru,brkgd->bukd", w_own, cotangent, preferred_element_type=f32)
    return output, dquery, dk_sh, dv_sh, dk_own, dv_own


def scatter_sum(x, axis_name, dim):
    n = lax.axis_size(axis_name)
    got = lax.all_to_all(x, axis_name, split_axis=dim, concat_axis=dim, tiled=True)
    shape = x.shape[:dim] + (n, x.shape[dim] // n) + x.shape[dim + 1 :]
    return jnp.sum(got.reshape(shape), axis=dim)


def all_gather_by_all_to_all(x, axis_name):
    n = lax.axis_size(axis_name)
    repeated = jnp.broadcast_to(x[None], (n,) + x.shape)
    return lax.all_to_all(repeated, axis_name, split_axis=0, concat_axis=0, tiled=True).reshape(
        (n * x.shape[0],) + x.shape[1:]
    )


def shift_perm(n, shift):
    return [(i, (i + shift) % n) for i in range(n)]


def body(prompt_q, prompt_kv, prompt_grad, resp_q, resp_kv, resp_grad, resp_prompt):
    head_size = HD
    block_rows = prompt_q.shape[1]
    kv_heads = prompt_q.shape[2]
    local_width = prompt_q.shape[3]
    local_heads = local_width // head_size
    full_len = block_rows * lax.axis_size("prompt")
    resp_len = resp_q.shape[3]
    peers = lax.axis_size("resp")
    kv_width = kv_heads * head_size
    q_width = kv_heads * local_width
    half = lax.dynamic_index_in_dim(prompt_kv[:, 0], lax.axis_index("head"), 0, keepdims=False)
    gathered_half = all_gather_by_all_to_all(half, "prompt")
    gathered = all_gather_by_all_to_all(gathered_half.reshape(1, full_len, kv_width), "head")
    prompt_keys = gathered[0].reshape(full_len, kv_heads, head_size)
    prompt_values = gathered[1].reshape(full_len, kv_heads, head_size)

    order = resp_prompt[0, 0]
    dest = (lax.axis_index("resp") + jnp.arange(peers)) % peers
    picker = (dest[:, None] == order[None, :]).astype(jnp.bfloat16)
    stacked = jnp.concatenate(
        [
            resp_q[0, 0].reshape(peers, resp_len, q_width),
            jnp.moveaxis(resp_kv[:, 0, 0], 0, 2).reshape(peers, resp_len, 2 * kv_width),
            resp_grad[0, 0].reshape(peers, resp_len, q_width),
        ],
        axis=-1,
    )
    send = jnp.einsum(
        "sj,jrh->srh", picker, stacked, preferred_element_type=jnp.float32
    ).astype(jnp.bfloat16)
    got = jnp.stack(
        [send[0]] + [lax.ppermute(send[s], "resp", shift_perm(peers, s)) for s in range(1, peers)]
    )
    got_q = got[..., :q_width]
    got_kv = jnp.moveaxis(
        got[..., q_width : q_width + 2 * kv_width].reshape(peers, resp_len, 2, kv_width), 2, 1
    )
    got_grad = got[..., q_width + 2 * kv_width :]

    q_shape = (peers + 1, resp_len, kv_heads, local_heads, head_size)
    queries = jnp.concatenate([got_q, prompt_q[0].reshape(1, resp_len, q_width)], axis=0).reshape(q_shape)
    cotangent = jnp.concatenate([got_grad, prompt_grad[0].reshape(1, resp_len, q_width)], axis=0).reshape(q_shape)
    own_kv = jnp.concatenate(
        [got_kv, jnp.zeros((1,) + got_kv.shape[1:], got_kv.dtype)], axis=0
    ).reshape(peers + 1, 2, resp_len, kv_heads, head_size)
    query_rows = lax.axis_index("prompt") * block_rows + jnp.arange(block_rows)
    key_cols = jnp.arange(full_len)
    causal = key_cols[None, :] <= query_rows[:, None]
    shared_ok = jnp.concatenate(
        [jnp.ones((peers, resp_len, full_len), bool), causal[None]], axis=0
    )
    steps_own = jnp.arange(resp_len)
    own_causal = steps_own[None, :] <= steps_own[:, None]
    own_ok = jnp.concatenate(
        [
            jnp.broadcast_to(own_causal, (peers, resp_len, resp_len)),
            jnp.zeros((1, resp_len, resp_len), bool),
        ],
        axis=0,
    )
    out, dq, dk_sh, dv_sh, dk_own, dv_own = attend_blocks(
        queries,
        prompt_keys,
        prompt_values,
        own_kv[:, 0],
        own_kv[:, 1],
        cotangent,
        shared_ok,
        own_ok,
    )
    out = out.reshape(peers + 1, resp_len, kv_heads, local_width)
    dq = dq.astype(jnp.bfloat16).reshape(peers + 1, resp_len, kv_heads, local_width)

    block_sum = jnp.stack(
        [
            scatter_sum(scatter_sum(part.reshape(full_len, kv_width), "head", 1), "prompt", 0)
            for part in (dk_sh, dv_sh)
        ]
    )
    own_part = jnp.stack([dk_own[:peers], dv_own[:peers]], axis=1).reshape(
        peers, 2, resp_len, kv_width
    )
    own_sum = scatter_sum(own_part, "head", 3)
    prompt_dkv = block_sum.astype(jnp.bfloat16)[:, None]
    back_kv = own_sum.astype(jnp.bfloat16)
    back = jnp.concatenate(
        [
            out[:peers].reshape(peers, resp_len, q_width),
            dq[:peers].reshape(peers, resp_len, q_width),
            jnp.moveaxis(back_kv, 1, 2).reshape(peers, resp_len, kv_width),
        ],
        axis=-1,
    )
    ret = jnp.stack(
        [back[0]]
        + [lax.ppermute(back[s], "resp", shift_perm(peers, -s)) for s in range(1, peers)]
    )
    mine = jnp.einsum(
        "sj,srh->jrh", picker, ret, preferred_element_type=jnp.float32
    ).astype(jnp.bfloat16)
    resp_out = mine[..., :q_width].reshape(peers, resp_len, kv_heads, local_width)[None, None]
    resp_dq = mine[..., q_width : 2 * q_width].reshape(
        peers, resp_len, kv_heads, local_width
    )[None, None]
    resp_dkv = jnp.moveaxis(
        mine[..., 2 * q_width :].reshape(peers, resp_len, 2, kv_width // 2), 2, 0
    )[:, None, None]
    prompt_out = out[peers:]
    prompt_dq = dq[peers:]
    return (prompt_out, prompt_dq, prompt_dkv, resp_out, resp_dq, resp_dkv)


def solution(mesh):
    return jax.shard_map(
        body,
        mesh=mesh,
        in_specs=(
            P("resp", "prompt", None, "head"),
            P(None, "resp", "prompt", None),
            P("resp", "prompt", None, "head"),
            P("prompt", "resp", None, None, None, "head"),
            P(None, "prompt", "resp", None, None, None),
            P("prompt", "resp", None, None, None, "head"),
            P("prompt", "resp", None),
        ),
        out_specs=(
            P("resp", "prompt", None, "head"),
            P("resp", "prompt", None, "head"),
            P(None, "resp", "prompt", "head"),
            P("prompt", "resp", None, None, None, "head"),
            P("prompt", "resp", None, None, None, "head"),
            P(None, "prompt", "resp", None, None, "head"),
        ),
        check_vma=False,
    )
```

```python
import math

import jax
import jax.numpy as jnp
from jax import lax
from jax.sharding import PartitionSpec as P

HD = 128


def attend_blocks(queries, keys_in, values_in, own_keys, own_values, cotangent, shared_ok, own_ok):
    scale = 1.0 / math.sqrt(HD)
    f32 = jnp.float32
    s_sh = jnp.einsum("brkgd,nkd->bkgrn", queries, keys_in, preferred_element_type=f32) * scale
    s_own = jnp.einsum("brkgd,bukd->bkgru", queries, own_keys, preferred_element_type=f32) * scale
    s_sh = jnp.where(shared_ok[:, None, None], s_sh, -1e30)
    s_own = jnp.where(own_ok[:, None, None], s_own, -1e30)
    row_max = jnp.maximum(
        jnp.max(s_sh, axis=-1, keepdims=True), jnp.max(s_own, axis=-1, keepdims=True)
    )
    totals = jnp.sum(jnp.exp(s_sh - row_max), axis=-1, keepdims=True) + jnp.sum(
        jnp.exp(s_own - row_max), axis=-1, keepdims=True
    )
    log_total = row_max + jnp.log(totals)
    p_sh = jnp.exp(s_sh - log_total)
    p_own = jnp.exp(s_own - log_total)
    w_sh = p_sh.astype(jnp.bfloat16)
    w_own = p_own.astype(jnp.bfloat16)
    output = (
        jnp.einsum("bkgrn,nkd->brkgd", w_sh, values_in, preferred_element_type=f32)
        + jnp.einsum("bkgru,bukd->brkgd", w_own, own_values, preferred_element_type=f32)
    ).astype(jnp.bfloat16)
    row_delta = jnp.einsum("brkgd,brkgd->bkgr", cotangent, output, preferred_element_type=f32)
    dp_sh = jnp.einsum("brkgd,nkd->bkgrn", cotangent, values_in, preferred_element_type=f32)
    dp_own = jnp.einsum("brkgd,bukd->bkgru", cotangent, own_values, preferred_element_type=f32)
    ds_sh = (p_sh * (dp_sh - row_delta[..., None])).astype(jnp.bfloat16)
    ds_own = (p_own * (dp_own - row_delta[..., None])).astype(jnp.bfloat16)
    dquery = (
        jnp.einsum("bkgrn,nkd->brkgd", ds_sh, keys_in, preferred_element_type=f32)
        + jnp.einsum("bkgru,bukd->brkgd", ds_own, own_keys, preferred_element_type=f32)
    ) * scale
    dk_sh = jnp.einsum("bkgrn,brkgd->nkd", ds_sh, queries, preferred_element_type=f32) * scale
    dv_sh = jnp.einsum("bkgrn,brkgd->nkd", w_sh, cotangent, preferred_element_type=f32)
    dk_own = jnp.einsum("bkgru,brkgd->bukd", ds_own, queries, preferred_element_type=f32) * scale
    dv_own = jnp.einsum("bkgru,brkgd->bukd", w_own, cotangent, preferred_element_type=f32)
    return output, dquery, dk_sh, dv_sh, dk_own, dv_own


def scatter_sum(x, axis_name, dim):
    n = lax.axis_size(axis_name)
    got = lax.all_to_all(x, axis_name, split_axis=dim, concat_axis=dim, tiled=True)
    shape = x.shape[:dim] + (n, x.shape[dim] // n) + x.shape[dim + 1 :]
    return jnp.sum(got.reshape(shape), axis=dim)


def all_gather_by_all_to_all(x, axis_name):
    n = lax.axis_size(axis_name)
    repeated = jnp.broadcast_to(x[None], (n,) + x.shape)
    return lax.all_to_all(repeated, axis_name, split_axis=0, concat_axis=0, tiled=True).reshape(
        (n * x.shape[0],) + x.shape[1:]
    )


def body(prompt_q, prompt_kv, prompt_grad, resp_q, resp_kv, resp_grad, resp_prompt):
    head_size = HD
    block_rows = prompt_q.shape[1]
    kv_heads = prompt_q.shape[2]
    local_width = prompt_q.shape[3]
    local_heads = local_width // head_size
    full_len = block_rows * lax.axis_size("prompt")
    resp_len = resp_q.shape[3]
    peers = lax.axis_size("resp")
    kv_width = kv_heads * head_size
    q_width = kv_heads * local_width
    half = lax.dynamic_index_in_dim(prompt_kv[:, 0], lax.axis_index("head"), 0, keepdims=False)
    gathered_half = lax.all_gather(half, "prompt", axis=0, tiled=True)

    def swap_halves(mine):
        both = all_gather_by_all_to_all(mine.reshape(1, full_len, kv_width), "head")
        return (
            both[0].reshape(full_len, kv_heads, head_size),
            both[1].reshape(full_len, kv_heads, head_size),
        )

    order = resp_prompt[0, 0]
    picker = (jnp.arange(peers)[:, None] == order[None, :]).astype(jnp.bfloat16)
    stacked = jnp.concatenate(
        [
            resp_q[0, 0].reshape(peers, resp_len, q_width),
            jnp.moveaxis(resp_kv[:, 0, 0], 0, 2).reshape(peers, resp_len, 2 * kv_width),
            resp_grad[0, 0].reshape(peers, resp_len, q_width),
        ],
        axis=-1,
    )
    send = jnp.einsum(
        "dj,jrh->drh", picker, stacked, preferred_element_type=jnp.float32
    ).astype(jnp.bfloat16)
    got = lax.all_to_all(send, "resp", split_axis=0, concat_axis=0, tiled=True)
    gathered_half, got = lax.optimization_barrier((gathered_half, got))
    prompt_keys, prompt_values = swap_halves(gathered_half)
    got_q = got[..., :q_width]
    got_kv = jnp.moveaxis(
        got[..., q_width : q_width + 2 * kv_width].reshape(peers, resp_len, 2, kv_width), 2, 1
    )
    got_grad = got[..., q_width + 2 * kv_width :]

    q_shape = (peers + 1, resp_len, kv_heads, local_heads, head_size)
    queries = jnp.concatenate([got_q, prompt_q[0].reshape(1, resp_len, q_width)], axis=0).reshape(q_shape)
    cotangent = jnp.concatenate([got_grad, prompt_grad[0].reshape(1, resp_len, q_width)], axis=0).reshape(q_shape)
    own_kv = jnp.concatenate(
        [got_kv, jnp.zeros((1,) + got_kv.shape[1:], got_kv.dtype)], axis=0
    ).reshape(peers + 1, 2, resp_len, kv_heads, head_size)
    query_rows = lax.axis_index("prompt") * block_rows + jnp.arange(block_rows)
    key_cols = jnp.arange(full_len)
    causal = key_cols[None, :] <= query_rows[:, None]
    shared_ok = jnp.concatenate(
        [jnp.ones((peers, resp_len, full_len), bool), causal[None]], axis=0
    )
    steps_own = jnp.arange(resp_len)
    own_causal = steps_own[None, :] <= steps_own[:, None]
    own_ok = jnp.concatenate(
        [
            jnp.broadcast_to(own_causal, (peers, resp_len, resp_len)),
            jnp.zeros((1, resp_len, resp_len), bool),
        ],
        axis=0,
    )
    out, dq, dk_sh, dv_sh, dk_own, dv_own = attend_blocks(
        queries,
        prompt_keys,
        prompt_values,
        own_kv[:, 0],
        own_kv[:, 1],
        cotangent,
        shared_ok,
        own_ok,
    )
    out = out.reshape(peers + 1, resp_len, kv_heads, local_width)
    dq = dq.astype(jnp.bfloat16).reshape(peers + 1, resp_len, kv_heads, local_width)

    block_sum = jnp.stack(
        [
            scatter_sum(scatter_sum(part.reshape(full_len, kv_width), "head", 1), "prompt", 0)
            for part in (dk_sh, dv_sh)
        ]
    )
    own_part = jnp.stack([dk_own[:peers], dv_own[:peers]], axis=1).reshape(
        peers, 2, resp_len, kv_width
    )
    own_sum = scatter_sum(own_part, "head", 3)
    prompt_dkv = block_sum.astype(jnp.bfloat16)[:, None]
    back_kv = own_sum.astype(jnp.bfloat16)
    back = jnp.concatenate(
        [
            out[:peers].reshape(peers, resp_len, q_width),
            dq[:peers].reshape(peers, resp_len, q_width),
            jnp.moveaxis(back_kv, 1, 2).reshape(peers, resp_len, kv_width),
        ],
        axis=-1,
    )
    ret = lax.all_to_all(back, "resp", split_axis=0, concat_axis=0, tiled=True)
    mine = jnp.einsum(
        "dj,drh->jrh", picker, ret, preferred_element_type=jnp.float32
    ).astype(jnp.bfloat16)
    resp_out = mine[..., :q_width].reshape(peers, resp_len, kv_heads, local_width)[None, None]
    resp_dq = mine[..., q_width : 2 * q_width].reshape(
        peers, resp_len, kv_heads, local_width
    )[None, None]
    resp_dkv = jnp.moveaxis(
        mine[..., 2 * q_width :].reshape(peers, resp_len, 2, kv_width // 2), 2, 0
    )[:, None, None]
    prompt_out = out[peers:]
    prompt_dq = dq[peers:]
    return (prompt_out, prompt_dq, prompt_dkv, resp_out, resp_dq, resp_dkv)


def solution(mesh):
    return jax.shard_map(
        body,
        mesh=mesh,
        in_specs=(
            P("resp", "prompt", None, "head"),
            P(None, "resp", "prompt", None),
            P("resp", "prompt", None, "head"),
            P("prompt", "resp", None, None, None, "head"),
            P(None, "prompt", "resp", None, None, None),
            P("prompt", "resp", None, None, None, "head"),
            P("prompt", "resp", None),
        ),
        out_specs=(
            P("resp", "prompt", None, "head"),
            P("resp", "prompt", None, "head"),
            P(None, "resp", "prompt", "head"),
            P("prompt", "resp", None, None, None, "head"),
            P("prompt", "resp", None, None, None, "head"),
            P(None, "prompt", "resp", None, None, "head"),
        ),
        check_vma=False,
    )
```

```python
import math

import jax
import jax.numpy as jnp
from jax import lax
from jax.sharding import PartitionSpec as P

HD = 128


def attend_blocks(queries, keys_in, values_in, own_keys, own_values, cotangent, shared_ok, own_ok):
    scale = 1.0 / math.sqrt(HD)
    f32 = jnp.float32
    s_sh = jnp.einsum("brkgd,nkd->bkgrn", queries, keys_in, preferred_element_type=f32) * scale
    s_own = jnp.einsum("brkgd,bukd->bkgru", queries, own_keys, preferred_element_type=f32) * scale
    s_sh = jnp.where(shared_ok[:, None, None], s_sh, -1e30)
    s_own = jnp.where(own_ok[:, None, None], s_own, -1e30)
    row_max = jnp.maximum(
        jnp.max(s_sh, axis=-1, keepdims=True), jnp.max(s_own, axis=-1, keepdims=True)
    )
    totals = jnp.sum(jnp.exp(s_sh - row_max), axis=-1, keepdims=True) + jnp.sum(
        jnp.exp(s_own - row_max), axis=-1, keepdims=True
    )
    log_total = row_max + jnp.log(totals)
    p_sh = jnp.exp(s_sh - log_total)
    p_own = jnp.exp(s_own - log_total)
    w_sh = p_sh.astype(jnp.bfloat16)
    w_own = p_own.astype(jnp.bfloat16)
    output = (
        jnp.einsum("bkgrn,nkd->brkgd", w_sh, values_in, preferred_element_type=f32)
        + jnp.einsum("bkgru,bukd->brkgd", w_own, own_values, preferred_element_type=f32)
    ).astype(jnp.bfloat16)
    row_delta = jnp.einsum("brkgd,brkgd->bkgr", cotangent, output, preferred_element_type=f32)
    dp_sh = jnp.einsum("brkgd,nkd->bkgrn", cotangent, values_in, preferred_element_type=f32)
    dp_own = jnp.einsum("brkgd,bukd->bkgru", cotangent, own_values, preferred_element_type=f32)
    ds_sh = (p_sh * (dp_sh - row_delta[..., None])).astype(jnp.bfloat16)
    ds_own = (p_own * (dp_own - row_delta[..., None])).astype(jnp.bfloat16)
    dquery = (
        jnp.einsum("bkgrn,nkd->brkgd", ds_sh, keys_in, preferred_element_type=f32)
        + jnp.einsum("bkgru,bukd->brkgd", ds_own, own_keys, preferred_element_type=f32)
    ) * scale
    dk_sh = jnp.einsum("bkgrn,brkgd->nkd", ds_sh, queries, preferred_element_type=f32) * scale
    dv_sh = jnp.einsum("bkgrn,brkgd->nkd", w_sh, cotangent, preferred_element_type=f32)
    dk_own = jnp.einsum("bkgru,brkgd->bukd", ds_own, queries, preferred_element_type=f32) * scale
    dv_own = jnp.einsum("bkgru,brkgd->bukd", w_own, cotangent, preferred_element_type=f32)
    return output, dquery, dk_sh, dv_sh, dk_own, dv_own


def scatter_sum(x, axis_name, dim):
    n = lax.axis_size(axis_name)
    got = lax.all_to_all(x, axis_name, split_axis=dim, concat_axis=dim, tiled=True)
    shape = x.shape[:dim] + (n, x.shape[dim] // n) + x.shape[dim + 1 :]
    return jnp.sum(got.reshape(shape), axis=dim)


def all_gather_by_all_to_all(x, axis_name):
    n = lax.axis_size(axis_name)
    repeated = jnp.broadcast_to(x[None], (n,) + x.shape)
    return lax.all_to_all(repeated, axis_name, split_axis=0, concat_axis=0, tiled=True).reshape(
        (n * x.shape[0],) + x.shape[1:]
    )


def body(prompt_q, prompt_kv, prompt_grad, resp_q, resp_kv, resp_grad, resp_prompt):
    head_size = HD
    block_rows = prompt_q.shape[1]
    kv_heads = prompt_q.shape[2]
    local_width = prompt_q.shape[3]
    local_heads = local_width // head_size
    full_len = block_rows * lax.axis_size("prompt")
    resp_len = resp_q.shape[3]
    peers = lax.axis_size("resp")
    kv_width = kv_heads * head_size
    q_width = kv_heads * local_width
    core = lax.axis_index("head")
    half = lax.dynamic_index_in_dim(prompt_kv[:, 0], core, 0, keepdims=False)
    gathered_half = all_gather_by_all_to_all(half, "prompt")

    order = resp_prompt[0, 0]
    picker = (jnp.arange(peers)[:, None] == order[None, :]).astype(jnp.bfloat16)
    stacked = jnp.concatenate(
        [
            resp_q[0, 0].reshape(peers, resp_len, q_width),
            lax.dynamic_index_in_dim(resp_kv[:, 0, 0], core, 0, keepdims=False),
            resp_grad[0, 0].reshape(peers, resp_len, q_width),
        ],
        axis=-1,
    )
    send = jnp.einsum(
        "dj,jrh->drh", picker, stacked, preferred_element_type=jnp.float32
    ).astype(jnp.bfloat16)
    got = lax.all_to_all(send, "resp", split_axis=0, concat_axis=0, tiled=True)
    got_q = got[..., :q_width]
    got_grad = got[..., q_width + kv_width :]
    mine = jnp.concatenate(
        [gathered_half, got[..., q_width : q_width + kv_width].reshape(peers * resp_len, kv_width)]
    )
    both = all_gather_by_all_to_all(mine[None], "head")
    prompt_keys = both[0, :full_len].reshape(full_len, kv_heads, head_size)
    prompt_values = both[1, :full_len].reshape(full_len, kv_heads, head_size)
    got_kv = both[:, full_len:].reshape(2, peers, resp_len, kv_width)
    got_kv = jnp.moveaxis(got_kv, 0, 1)

    q_shape = (peers + 1, resp_len, kv_heads, local_heads, head_size)
    queries = jnp.concatenate([got_q, prompt_q[0].reshape(1, resp_len, q_width)], axis=0).reshape(q_shape)
    cotangent = jnp.concatenate([got_grad, prompt_grad[0].reshape(1, resp_len, q_width)], axis=0).reshape(q_shape)
    own_kv = jnp.concatenate(
        [got_kv, jnp.zeros((1,) + got_kv.shape[1:], got_kv.dtype)], axis=0
    ).reshape(peers + 1, 2, resp_len, kv_heads, head_size)
    query_rows = lax.axis_index("prompt") * block_rows + jnp.arange(block_rows)
    key_cols = jnp.arange(full_len)
    causal = key_cols[None, :] <= query_rows[:, None]
    shared_ok = jnp.concatenate(
        [jnp.ones((peers, resp_len, full_len), bool), causal[None]], axis=0
    )
    steps_own = jnp.arange(resp_len)
    own_causal = steps_own[None, :] <= steps_own[:, None]
    own_ok = jnp.concatenate(
        [
            jnp.broadcast_to(own_causal, (peers, resp_len, resp_len)),
            jnp.zeros((1, resp_len, resp_len), bool),
        ],
        axis=0,
    )
    out, dq, dk_sh, dv_sh, dk_own, dv_own = attend_blocks(
        queries,
        prompt_keys,
        prompt_values,
        own_kv[:, 0],
        own_kv[:, 1],
        cotangent,
        shared_ok,
        own_ok,
    )
    out = out.reshape(peers + 1, resp_len, kv_heads, local_width)
    dq = dq.astype(jnp.bfloat16).reshape(peers + 1, resp_len, kv_heads, local_width)

    prompt_rows = 2 * full_len
    partials = jnp.concatenate(
        [
            jnp.stack([dk_sh, dv_sh]).reshape(prompt_rows, kv_width),
            jnp.stack([dk_own[:peers], dv_own[:peers]], axis=1).reshape(-1, kv_width),
        ]
    )
    head_sum = scatter_sum(partials, "head", 1)
    block_sum = scatter_sum(head_sum[:prompt_rows].reshape(2, full_len, -1), "prompt", 1)
    own_sum = head_sum[prompt_rows:].reshape(peers, 2, resp_len, -1)
    prompt_dkv = block_sum.astype(jnp.bfloat16)[:, None]
    back_kv = own_sum.astype(jnp.bfloat16)
    back = jnp.concatenate(
        [
            out[:peers].reshape(peers, resp_len, q_width),
            dq[:peers].reshape(peers, resp_len, q_width),
            jnp.moveaxis(back_kv, 1, 2).reshape(peers, resp_len, kv_width),
        ],
        axis=-1,
    )
    ret = lax.all_to_all(back, "resp", split_axis=0, concat_axis=0, tiled=True)
    mine = jnp.einsum(
        "dj,drh->jrh", picker, ret, preferred_element_type=jnp.float32
    ).astype(jnp.bfloat16)
    resp_out = mine[..., :q_width].reshape(peers, resp_len, kv_heads, local_width)[None, None]
    resp_dq = mine[..., q_width : 2 * q_width].reshape(
        peers, resp_len, kv_heads, local_width
    )[None, None]
    resp_dkv = jnp.moveaxis(
        mine[..., 2 * q_width :].reshape(peers, resp_len, 2, kv_width // 2), 2, 0
    )[:, None, None]
    prompt_out = out[peers:]
    prompt_dq = dq[peers:]
    return (prompt_out, prompt_dq, prompt_dkv, resp_out, resp_dq, resp_dkv)


def solution(mesh):
    return jax.shard_map(
        body,
        mesh=mesh,
        in_specs=(
            P("resp", "prompt", None, "head"),
            P(None, "resp", "prompt", None),
            P("resp", "prompt", None, "head"),
            P("prompt", "resp", None, None, None, "head"),
            P(None, "prompt", "resp", None, None, None),
            P("prompt", "resp", None, None, None, "head"),
            P("prompt", "resp", None),
        ),
        out_specs=(
            P("resp", "prompt", None, "head"),
            P("resp", "prompt", None, "head"),
            P(None, "resp", "prompt", "head"),
            P("prompt", "resp", None, None, None, "head"),
            P("prompt", "resp", None, None, None, "head"),
            P(None, "prompt", "resp", None, None, "head"),
        ),
        check_vma=False,
    )
```

```python
import math

import jax
import jax.numpy as jnp
from jax import lax
from jax.sharding import PartitionSpec as P

HD = 128


def attend_blocks(queries, keys_in, values_in, own_keys, own_values, cotangent, shared_ok, own_ok):
    scale = 1.0 / math.sqrt(HD)
    f32 = jnp.float32
    s_sh = jnp.einsum("brkgd,nkd->bkgrn", queries, keys_in, preferred_element_type=f32) * scale
    s_own = jnp.einsum("brkgd,bukd->bkgru", queries, own_keys, preferred_element_type=f32) * scale
    s_sh = jnp.where(shared_ok[:, None, None], s_sh, -1e30)
    s_own = jnp.where(own_ok[:, None, None], s_own, -1e30)
    row_max = jnp.maximum(
        jnp.max(s_sh, axis=-1, keepdims=True), jnp.max(s_own, axis=-1, keepdims=True)
    )
    totals = jnp.sum(jnp.exp(s_sh - row_max), axis=-1, keepdims=True) + jnp.sum(
        jnp.exp(s_own - row_max), axis=-1, keepdims=True
    )
    log_total = row_max + jnp.log(totals)
    p_sh = jnp.exp(s_sh - log_total)
    p_own = jnp.exp(s_own - log_total)
    w_sh = p_sh.astype(jnp.bfloat16)
    w_own = p_own.astype(jnp.bfloat16)
    output = (
        jnp.einsum("bkgrn,nkd->brkgd", w_sh, values_in, preferred_element_type=f32)
        + jnp.einsum("bkgru,bukd->brkgd", w_own, own_values, preferred_element_type=f32)
    ).astype(jnp.bfloat16)
    row_delta = jnp.einsum("brkgd,brkgd->bkgr", cotangent, output, preferred_element_type=f32)
    dp_sh = jnp.einsum("brkgd,nkd->bkgrn", cotangent, values_in, preferred_element_type=f32)
    dp_own = jnp.einsum("brkgd,bukd->bkgru", cotangent, own_values, preferred_element_type=f32)
    ds_sh = (p_sh * (dp_sh - row_delta[..., None])).astype(jnp.bfloat16)
    ds_own = (p_own * (dp_own - row_delta[..., None])).astype(jnp.bfloat16)
    dquery = (
        jnp.einsum("bkgrn,nkd->brkgd", ds_sh, keys_in, preferred_element_type=f32)
        + jnp.einsum("bkgru,bukd->brkgd", ds_own, own_keys, preferred_element_type=f32)
    ) * scale
    dk_sh = jnp.einsum("bkgrn,brkgd->knd", ds_sh, queries, preferred_element_type=f32) * scale
    dv_sh = jnp.einsum("bkgrn,brkgd->knd", w_sh, cotangent, preferred_element_type=f32)
    dk_own = jnp.einsum("bkgru,brkgd->kbud", ds_own, queries, preferred_element_type=f32) * scale
    dv_own = jnp.einsum("bkgru,brkgd->kbud", w_own, cotangent, preferred_element_type=f32)
    return output, dquery, dk_sh, dv_sh, dk_own, dv_own


def scatter_sum(x, axis_name, dim):
    n = lax.axis_size(axis_name)
    got = lax.all_to_all(x, axis_name, split_axis=dim, concat_axis=dim, tiled=True)
    shape = x.shape[:dim] + (n, x.shape[dim] // n) + x.shape[dim + 1 :]
    return jnp.sum(got.reshape(shape), axis=dim)


def all_gather_by_all_to_all(x, axis_name):
    n = lax.axis_size(axis_name)
    repeated = jnp.broadcast_to(x[None], (n,) + x.shape)
    return lax.all_to_all(repeated, axis_name, split_axis=0, concat_axis=0, tiled=True).reshape(
        (n * x.shape[0],) + x.shape[1:]
    )


def body(prompt_q, prompt_kv, prompt_grad, resp_q, resp_kv, resp_grad, resp_prompt):
    head_size = HD
    block_rows = prompt_q.shape[1]
    kv_heads = prompt_q.shape[2]
    local_width = prompt_q.shape[3]
    local_heads = local_width // head_size
    full_len = block_rows * lax.axis_size("prompt")
    resp_len = resp_q.shape[3]
    peers = lax.axis_size("resp")
    kv_width = kv_heads * head_size
    q_width = kv_heads * local_width
    half = lax.dynamic_index_in_dim(prompt_kv[:, 0], lax.axis_index("head"), 0, keepdims=False)
    gathered_half = all_gather_by_all_to_all(half, "prompt")
    gathered = all_gather_by_all_to_all(gathered_half.reshape(1, full_len, kv_width), "head")
    prompt_keys = gathered[0].reshape(full_len, kv_heads, head_size)
    prompt_values = gathered[1].reshape(full_len, kv_heads, head_size)

    order = resp_prompt[0, 0]
    picker = (jnp.arange(peers)[:, None] == order[None, :]).astype(jnp.bfloat16)
    stacked = jnp.concatenate(
        [
            resp_q[0, 0].reshape(peers, resp_len, q_width),
            jnp.moveaxis(resp_kv[:, 0, 0], 0, 2).reshape(peers, resp_len, 2 * kv_width),
            resp_grad[0, 0].reshape(peers, resp_len, q_width),
        ],
        axis=-1,
    )
    send = jnp.einsum(
        "dj,jrh->drh", picker, stacked, preferred_element_type=jnp.float32
    ).astype(jnp.bfloat16)
    got = lax.all_to_all(send, "resp", split_axis=0, concat_axis=0, tiled=True)
    got_q = got[..., :q_width]
    got_kv = jnp.moveaxis(
        got[..., q_width : q_width + 2 * kv_width].reshape(peers, resp_len, 2, kv_width), 2, 1
    )
    got_grad = got[..., q_width + 2 * kv_width :]

    q_shape = (peers + 1, resp_len, kv_heads, local_heads, head_size)
    queries = jnp.concatenate([got_q, prompt_q[0].reshape(1, resp_len, q_width)], axis=0).reshape(q_shape)
    cotangent = jnp.concatenate([got_grad, prompt_grad[0].reshape(1, resp_len, q_width)], axis=0).reshape(q_shape)
    own_kv = jnp.concatenate(
        [got_kv, jnp.zeros((1,) + got_kv.shape[1:], got_kv.dtype)], axis=0
    ).reshape(peers + 1, 2, resp_len, kv_heads, head_size)
    query_rows = lax.axis_index("prompt") * block_rows + jnp.arange(block_rows)
    key_cols = jnp.arange(full_len)
    causal = key_cols[None, :] <= query_rows[:, None]
    shared_ok = jnp.concatenate(
        [jnp.ones((peers, resp_len, full_len), bool), causal[None]], axis=0
    )
    steps_own = jnp.arange(resp_len)
    own_causal = steps_own[None, :] <= steps_own[:, None]
    own_ok = jnp.concatenate(
        [
            jnp.broadcast_to(own_causal, (peers, resp_len, resp_len)),
            jnp.zeros((1, resp_len, resp_len), bool),
        ],
        axis=0,
    )
    out, dq, dk_sh, dv_sh, dk_own, dv_own = attend_blocks(
        queries,
        prompt_keys,
        prompt_values,
        own_kv[:, 0],
        own_kv[:, 1],
        cotangent,
        shared_ok,
        own_ok,
    )
    out = out.reshape(peers + 1, resp_len, kv_heads, local_width)
    dq = dq.astype(jnp.bfloat16).reshape(peers + 1, resp_len, kv_heads, local_width)

    n_blocks = lax.axis_size("prompt")
    local_kv = kv_heads // lax.axis_size("head")

    def block_sum_of(part):
        mine = scatter_sum(part, "head", 0).reshape(local_kv, n_blocks, block_rows, head_size)
        got_blocks = lax.all_to_all(
            jnp.moveaxis(mine, 1, 0), "prompt", split_axis=0, concat_axis=0, tiled=True
        )
        total = jnp.sum(got_blocks, axis=0)
        return jnp.moveaxis(total, 0, 1).reshape(block_rows, local_kv * head_size)

    block_sum = jnp.stack([block_sum_of(dk_sh), block_sum_of(dv_sh)])
    own_sum = scatter_sum(jnp.stack([dk_own[:, :peers], dv_own[:, :peers]], axis=1), "head", 0)
    back_kv = (
        jnp.transpose(own_sum, (2, 3, 1, 0, 4))
        .reshape(peers, resp_len, 2 * local_kv * head_size)
        .astype(jnp.bfloat16)
    )
    prompt_dkv = block_sum.astype(jnp.bfloat16)[:, None]
    back = jnp.concatenate(
        [
            out[:peers].reshape(peers, resp_len, q_width),
            dq[:peers].reshape(peers, resp_len, q_width),
            back_kv,
        ],
        axis=-1,
    )
    ret = lax.all_to_all(back, "resp", split_axis=0, concat_axis=0, tiled=True)
    mine = jnp.einsum(
        "dj,drh->jrh", picker, ret, preferred_element_type=jnp.float32
    ).astype(jnp.bfloat16)
    resp_out = mine[..., :q_width].reshape(peers, resp_len, kv_heads, local_width)[None, None]
    resp_dq = mine[..., q_width : 2 * q_width].reshape(
        peers, resp_len, kv_heads, local_width
    )[None, None]
    resp_dkv = jnp.moveaxis(
        mine[..., 2 * q_width :].reshape(peers, resp_len, 2, kv_width // 2), 2, 0
    )[:, None, None]
    prompt_out = out[peers:]
    prompt_dq = dq[peers:]
    return (prompt_out, prompt_dq, prompt_dkv, resp_out, resp_dq, resp_dkv)


def solution(mesh):
    return jax.shard_map(
        body,
        mesh=mesh,
        in_specs=(
            P("resp", "prompt", None, "head"),
            P(None, "resp", "prompt", None),
            P("resp", "prompt", None, "head"),
            P("prompt", "resp", None, None, None, "head"),
            P(None, "prompt", "resp", None, None, None),
            P("prompt", "resp", None, None, None, "head"),
            P("prompt", "resp", None),
        ),
        out_specs=(
            P("resp", "prompt", None, "head"),
            P("resp", "prompt", None, "head"),
            P(None, "resp", "prompt", "head"),
            P("prompt", "resp", None, None, None, "head"),
            P("prompt", "resp", None, None, None, "head"),
            P(None, "prompt", "resp", None, None, "head"),
        ),
        check_vma=False,
    )
```

```python
import math

import jax
import jax.numpy as jnp
from jax import lax
from jax.sharding import PartitionSpec as P

HD = 128


def attend_blocks(queries, keys_in, values_in, own_keys, own_values, cotangent, shared_ok, own_ok):
    scale = 1.0 / math.sqrt(HD)
    f32 = jnp.float32
    s_sh = jnp.einsum("brkgd,nkd->bkgrn", queries, keys_in, preferred_element_type=f32) * scale
    s_own = jnp.einsum("brkgd,bukd->bkgru", queries, own_keys, preferred_element_type=f32) * scale
    s_sh = jnp.where(shared_ok[:, None, None], s_sh, -1e30)
    s_own = jnp.where(own_ok[:, None, None], s_own, -1e30)
    row_max = jnp.maximum(
        jnp.max(s_sh, axis=-1, keepdims=True), jnp.max(s_own, axis=-1, keepdims=True)
    )
    totals = jnp.sum(jnp.exp(s_sh - row_max), axis=-1, keepdims=True) + jnp.sum(
        jnp.exp(s_own - row_max), axis=-1, keepdims=True
    )
    log_total = row_max + jnp.log(totals)
    p_sh = jnp.exp(s_sh - log_total)
    p_own = jnp.exp(s_own - log_total)
    w_sh = p_sh.astype(jnp.bfloat16)
    w_own = p_own.astype(jnp.bfloat16)
    output = (
        jnp.einsum("bkgrn,nkd->brkgd", w_sh, values_in, preferred_element_type=f32)
        + jnp.einsum("bkgru,bukd->brkgd", w_own, own_values, preferred_element_type=f32)
    ).astype(jnp.bfloat16)
    row_delta = jnp.einsum("brkgd,brkgd->bkgr", cotangent, output, preferred_element_type=f32)
    dp_sh = jnp.einsum("brkgd,nkd->bkgrn", cotangent, values_in, preferred_element_type=f32)
    dp_own = jnp.einsum("brkgd,bukd->bkgru", cotangent, own_values, preferred_element_type=f32)
    ds_sh = (p_sh * (dp_sh - row_delta[..., None])).astype(jnp.bfloat16)
    ds_own = (p_own * (dp_own - row_delta[..., None])).astype(jnp.bfloat16)
    dquery = (
        jnp.einsum("bkgrn,nkd->brkgd", ds_sh, keys_in, preferred_element_type=f32)
        + jnp.einsum("bkgru,bukd->brkgd", ds_own, own_keys, preferred_element_type=f32)
    ) * scale
    dk_sh = jnp.einsum("bkgrn,brkgd->knd", ds_sh, queries, preferred_element_type=f32) * scale
    dv_sh = jnp.einsum("bkgrn,brkgd->knd", w_sh, cotangent, preferred_element_type=f32)
    dk_own = jnp.einsum("bkgru,brkgd->kbud", ds_own, queries, preferred_element_type=f32) * scale
    dv_own = jnp.einsum("bkgru,brkgd->kbud", w_own, cotangent, preferred_element_type=f32)
    return output, dquery, dk_sh, dv_sh, dk_own, dv_own


def scatter_sum(x, axis_name, dim):
    n = lax.axis_size(axis_name)
    got = lax.all_to_all(x, axis_name, split_axis=dim, concat_axis=dim, tiled=True)
    shape = x.shape[:dim] + (n, x.shape[dim] // n) + x.shape[dim + 1 :]
    return jnp.sum(got.reshape(shape), axis=dim)


def all_gather_by_all_to_all(x, axis_name):
    n = lax.axis_size(axis_name)
    repeated = jnp.broadcast_to(x[None], (n,) + x.shape)
    return lax.all_to_all(repeated, axis_name, split_axis=0, concat_axis=0, tiled=True).reshape(
        (n * x.shape[0],) + x.shape[1:]
    )


def body(prompt_q, prompt_kv, prompt_grad, resp_q, resp_kv, resp_grad, resp_prompt):
    head_size = HD
    block_rows = prompt_q.shape[1]
    kv_heads = prompt_q.shape[2]
    local_width = prompt_q.shape[3]
    local_heads = local_width // head_size
    full_len = block_rows * lax.axis_size("prompt")
    resp_len = resp_q.shape[3]
    peers = lax.axis_size("resp")
    kv_width = kv_heads * head_size
    q_width = kv_heads * local_width
    half = lax.dynamic_index_in_dim(prompt_kv[:, 0], lax.axis_index("head"), 0, keepdims=False)
    gathered_half = all_gather_by_all_to_all(half, "prompt")
    gathered = all_gather_by_all_to_all(gathered_half.reshape(1, full_len, kv_width), "head")
    prompt_keys = gathered[0].reshape(full_len, kv_heads, head_size)
    prompt_values = gathered[1].reshape(full_len, kv_heads, head_size)

    order = resp_prompt[0, 0]
    picker = (jnp.arange(peers)[:, None] == order[None, :]).astype(jnp.bfloat16)
    stacked = jnp.concatenate(
        [
            resp_q[0, 0].reshape(peers, resp_len, q_width),
            jnp.moveaxis(resp_kv[:, 0, 0], 0, 2).reshape(peers, resp_len, 2 * kv_width),
            resp_grad[0, 0].reshape(peers, resp_len, q_width),
        ],
        axis=-1,
    )
    send = jnp.einsum(
        "dj,jrh->drh", picker, stacked, preferred_element_type=jnp.float32
    ).astype(jnp.bfloat16)
    got = lax.all_to_all(send, "resp", split_axis=0, concat_axis=0, tiled=True)
    got_q = got[..., :q_width]
    got_kv = jnp.moveaxis(
        got[..., q_width : q_width + 2 * kv_width].reshape(peers, resp_len, 2, kv_width), 2, 1
    )
    got_grad = got[..., q_width + 2 * kv_width :]

    q_shape = (peers + 1, resp_len, kv_heads, local_heads, head_size)
    queries = jnp.concatenate([got_q, prompt_q[0].reshape(1, resp_len, q_width)], axis=0).reshape(q_shape)
    cotangent = jnp.concatenate([got_grad, prompt_grad[0].reshape(1, resp_len, q_width)], axis=0).reshape(q_shape)
    own_kv = jnp.concatenate(
        [got_kv, jnp.zeros((1,) + got_kv.shape[1:], got_kv.dtype)], axis=0
    ).reshape(peers + 1, 2, resp_len, kv_heads, head_size)
    query_rows = lax.axis_index("prompt") * block_rows + jnp.arange(block_rows)
    key_cols = jnp.arange(full_len)
    causal = key_cols[None, :] <= query_rows[:, None]
    shared_ok = jnp.concatenate(
        [jnp.ones((peers, resp_len, full_len), bool), causal[None]], axis=0
    )
    steps_own = jnp.arange(resp_len)
    own_causal = steps_own[None, :] <= steps_own[:, None]
    own_ok = jnp.concatenate(
        [
            jnp.broadcast_to(own_causal, (peers, resp_len, resp_len)),
            jnp.zeros((1, resp_len, resp_len), bool),
        ],
        axis=0,
    )
    out, dq, dk_sh, dv_sh, dk_own, dv_own = attend_blocks(
        queries,
        prompt_keys,
        prompt_values,
        own_kv[:, 0],
        own_kv[:, 1],
        cotangent,
        shared_ok,
        own_ok,
    )
    out = out.reshape(peers + 1, resp_len, kv_heads, local_width)
    dq = dq.astype(jnp.bfloat16).reshape(peers + 1, resp_len, kv_heads, local_width)

    n_blocks = lax.axis_size("prompt")
    local_kv = kv_heads // lax.axis_size("head")

    both_parts = jnp.stack([dk_sh, dv_sh], axis=1)
    mine = scatter_sum(both_parts, "head", 0).reshape(local_kv, 2, n_blocks, block_rows, head_size)
    got_blocks = lax.all_to_all(
        jnp.moveaxis(mine, 2, 0), "prompt", split_axis=0, concat_axis=0, tiled=True
    )
    total = jnp.sum(got_blocks, axis=0)
    block_sum = jnp.transpose(total, (1, 2, 0, 3)).reshape(2, block_rows, local_kv * head_size)
    own_sum = scatter_sum(jnp.stack([dk_own[:, :peers], dv_own[:, :peers]], axis=1), "head", 0)
    back_kv = (
        jnp.transpose(own_sum, (2, 3, 1, 0, 4))
        .reshape(peers, resp_len, 2 * local_kv * head_size)
        .astype(jnp.bfloat16)
    )
    prompt_dkv = block_sum.astype(jnp.bfloat16)[:, None]
    back = jnp.concatenate(
        [
            out[:peers].reshape(peers, resp_len, q_width),
            dq[:peers].reshape(peers, resp_len, q_width),
            back_kv,
        ],
        axis=-1,
    )
    ret = lax.all_to_all(back, "resp", split_axis=0, concat_axis=0, tiled=True)
    mine = jnp.einsum(
        "dj,drh->jrh", picker, ret, preferred_element_type=jnp.float32
    ).astype(jnp.bfloat16)
    resp_out = mine[..., :q_width].reshape(peers, resp_len, kv_heads, local_width)[None, None]
    resp_dq = mine[..., q_width : 2 * q_width].reshape(
        peers, resp_len, kv_heads, local_width
    )[None, None]
    resp_dkv = jnp.moveaxis(
        mine[..., 2 * q_width :].reshape(peers, resp_len, 2, kv_width // 2), 2, 0
    )[:, None, None]
    prompt_out = out[peers:]
    prompt_dq = dq[peers:]
    return (prompt_out, prompt_dq, prompt_dkv, resp_out, resp_dq, resp_dkv)


def solution(mesh):
    return jax.shard_map(
        body,
        mesh=mesh,
        in_specs=(
            P("resp", "prompt", None, "head"),
            P(None, "resp", "prompt", None),
            P("resp", "prompt", None, "head"),
            P("prompt", "resp", None, None, None, "head"),
            P(None, "prompt", "resp", None, None, None),
            P("prompt", "resp", None, None, None, "head"),
            P("prompt", "resp", None),
        ),
        out_specs=(
            P("resp", "prompt", None, "head"),
            P("resp", "prompt", None, "head"),
            P(None, "resp", "prompt", "head"),
            P("prompt", "resp", None, None, None, "head"),
            P("prompt", "resp", None, None, None, "head"),
            P(None, "prompt", "resp", None, None, "head"),
        ),
        check_vma=False,
    )
```

```python
import math

import jax
import jax.numpy as jnp
from jax import lax
from jax.sharding import PartitionSpec as P

HD = 128


def attend_blocks(
    queries, keys_in, values_in, own_keys, own_values, cotangent, shared_limit, own_limit
):
    scale = 1.0 / math.sqrt(HD)
    f32 = jnp.float32
    s_sh = jnp.einsum("brkgd,nkd->bkgrn", queries, keys_in, preferred_element_type=f32) * scale
    s_own = jnp.einsum("brkgd,bukd->bkgru", queries, own_keys, preferred_element_type=f32) * scale
    shared_ok = lax.broadcasted_iota(jnp.int32, s_sh.shape, 4) <= shared_limit[:, None, None, :, None]
    own_ok = lax.broadcasted_iota(jnp.int32, s_own.shape, 4) <= own_limit[:, None, None, :, None]
    s_sh = jnp.where(shared_ok, s_sh, -1e30)
    s_own = jnp.where(own_ok, s_own, -1e30)
    row_max = jnp.maximum(
        jnp.max(s_sh, axis=-1, keepdims=True), jnp.max(s_own, axis=-1, keepdims=True)
    )
    totals = jnp.sum(jnp.exp(s_sh - row_max), axis=-1, keepdims=True) + jnp.sum(
        jnp.exp(s_own - row_max), axis=-1, keepdims=True
    )
    log_total = row_max + jnp.log(totals)
    p_sh = jnp.exp(s_sh - log_total)
    p_own = jnp.exp(s_own - log_total)
    w_sh = p_sh.astype(jnp.bfloat16)
    w_own = p_own.astype(jnp.bfloat16)
    output = (
        jnp.einsum("bkgrn,nkd->brkgd", w_sh, values_in, preferred_element_type=f32)
        + jnp.einsum("bkgru,bukd->brkgd", w_own, own_values, preferred_element_type=f32)
    ).astype(jnp.bfloat16)
    row_delta = jnp.einsum("brkgd,brkgd->bkgr", cotangent, output, preferred_element_type=f32)
    dp_sh = jnp.einsum("brkgd,nkd->bkgrn", cotangent, values_in, preferred_element_type=f32)
    dp_own = jnp.einsum("brkgd,bukd->bkgru", cotangent, own_values, preferred_element_type=f32)
    ds_sh = (p_sh * (dp_sh - row_delta[..., None])).astype(jnp.bfloat16)
    ds_own = (p_own * (dp_own - row_delta[..., None])).astype(jnp.bfloat16)
    dquery = (
        jnp.einsum("bkgrn,nkd->brkgd", ds_sh, keys_in, preferred_element_type=f32)
        + jnp.einsum("bkgru,bukd->brkgd", ds_own, own_keys, preferred_element_type=f32)
    ) * scale
    dk_sh = jnp.einsum("bkgrn,brkgd->knd", ds_sh, queries, preferred_element_type=f32) * scale
    dv_sh = jnp.einsum("bkgrn,brkgd->knd", w_sh, cotangent, preferred_element_type=f32)
    dk_own = jnp.einsum("bkgru,brkgd->kbud", ds_own, queries, preferred_element_type=f32) * scale
    dv_own = jnp.einsum("bkgru,brkgd->kbud", w_own, cotangent, preferred_element_type=f32)
    return output, dquery, dk_sh, dv_sh, dk_own, dv_own


def scatter_sum(x, axis_name, dim):
    n = lax.axis_size(axis_name)
    got = lax.all_to_all(x, axis_name, split_axis=dim, concat_axis=dim, tiled=True)
    shape = x.shape[:dim] + (n, x.shape[dim] // n) + x.shape[dim + 1 :]
    return jnp.sum(got.reshape(shape), axis=dim)


def all_gather_by_all_to_all(x, axis_name):
    n = lax.axis_size(axis_name)
    repeated = jnp.broadcast_to(x[None], (n,) + x.shape)
    return lax.all_to_all(repeated, axis_name, split_axis=0, concat_axis=0, tiled=True).reshape(
        (n * x.shape[0],) + x.shape[1:]
    )


def body(prompt_q, prompt_kv, prompt_grad, resp_q, resp_kv, resp_grad, resp_prompt):
    head_size = HD
    block_rows = prompt_q.shape[1]
    kv_heads = prompt_q.shape[2]
    local_width = prompt_q.shape[3]
    local_heads = local_width // head_size
    full_len = block_rows * lax.axis_size("prompt")
    resp_len = resp_q.shape[3]
    peers = lax.axis_size("resp")
    kv_width = kv_heads * head_size
    q_width = kv_heads * local_width
    half = lax.dynamic_index_in_dim(prompt_kv[:, 0], lax.axis_index("head"), 0, keepdims=False)
    gathered_half = all_gather_by_all_to_all(half, "prompt")
    gathered = all_gather_by_all_to_all(gathered_half.reshape(1, full_len, kv_width), "head")
    prompt_keys = gathered[0].reshape(full_len, kv_heads, head_size)
    prompt_values = gathered[1].reshape(full_len, kv_heads, head_size)

    order = resp_prompt[0, 0]
    picker = (jnp.arange(peers)[:, None] == order[None, :]).astype(jnp.bfloat16)
    stacked = jnp.concatenate(
        [
            resp_q[0, 0].reshape(peers, resp_len, q_width),
            jnp.moveaxis(resp_kv[:, 0, 0], 0, 2).reshape(peers, resp_len, 2 * kv_width),
            resp_grad[0, 0].reshape(peers, resp_len, q_width),
        ],
        axis=-1,
    )
    send = jnp.einsum(
        "dj,jrh->drh", picker, stacked, preferred_element_type=jnp.float32
    ).astype(jnp.bfloat16)
    got = lax.all_to_all(send, "resp", split_axis=0, concat_axis=0, tiled=True)
    got_q = got[..., :q_width]
    got_kv = jnp.moveaxis(
        got[..., q_width : q_width + 2 * kv_width].reshape(peers, resp_len, 2, kv_width), 2, 1
    )
    got_grad = got[..., q_width + 2 * kv_width :]

    q_shape = (peers + 1, resp_len, kv_heads, local_heads, head_size)
    queries = jnp.concatenate([got_q, prompt_q[0].reshape(1, resp_len, q_width)], axis=0).reshape(q_shape)
    cotangent = jnp.concatenate([got_grad, prompt_grad[0].reshape(1, resp_len, q_width)], axis=0).reshape(q_shape)
    own_kv = jnp.concatenate(
        [got_kv, jnp.zeros((1,) + got_kv.shape[1:], got_kv.dtype)], axis=0
    ).reshape(peers + 1, 2, resp_len, kv_heads, head_size)
    query_rows = lax.axis_index("prompt") * block_rows + jnp.arange(block_rows)
    steps_own = jnp.arange(resp_len)
    shared_limit = jnp.concatenate(
        [jnp.full((peers, resp_len), full_len, jnp.int32), query_rows[None].astype(jnp.int32)]
    )
    own_limit = jnp.concatenate(
        [
            jnp.broadcast_to(steps_own, (peers, resp_len)).astype(jnp.int32),
            jnp.full((1, resp_len), -1, jnp.int32),
        ]
    )
    out, dq, dk_sh, dv_sh, dk_own, dv_own = attend_blocks(
        queries,
        prompt_keys,
        prompt_values,
        own_kv[:, 0],
        own_kv[:, 1],
        cotangent,
        shared_limit,
        own_limit,
    )
    out = out.reshape(peers + 1, resp_len, kv_heads, local_width)
    dq = dq.astype(jnp.bfloat16).reshape(peers + 1, resp_len, kv_heads, local_width)

    n_blocks = lax.axis_size("prompt")
    local_kv = kv_heads // lax.axis_size("head")

    both_parts = jnp.stack([dk_sh, dv_sh], axis=1)
    mine = scatter_sum(both_parts, "head", 0).reshape(local_kv, 2, n_blocks, block_rows, head_size)
    got_blocks = lax.all_to_all(
        jnp.moveaxis(mine, 2, 0), "prompt", split_axis=0, concat_axis=0, tiled=True
    )
    total = jnp.sum(got_blocks, axis=0)
    block_sum = jnp.transpose(total, (1, 2, 0, 3)).reshape(2, block_rows, local_kv * head_size)
    own_sum = scatter_sum(jnp.stack([dk_own[:, :peers], dv_own[:, :peers]], axis=1), "head", 0)
    back_kv = (
        jnp.transpose(own_sum, (2, 3, 1, 0, 4))
        .reshape(peers, resp_len, 2 * local_kv * head_size)
        .astype(jnp.bfloat16)
    )
    prompt_dkv = block_sum.astype(jnp.bfloat16)[:, None]
    back = jnp.concatenate(
        [
            out[:peers].reshape(peers, resp_len, q_width),
            dq[:peers].reshape(peers, resp_len, q_width),
            back_kv,
        ],
        axis=-1,
    )
    ret = lax.all_to_all(back, "resp", split_axis=0, concat_axis=0, tiled=True)
    mine = jnp.einsum(
        "dj,drh->jrh", picker, ret, preferred_element_type=jnp.float32
    ).astype(jnp.bfloat16)
    resp_out = mine[..., :q_width].reshape(peers, resp_len, kv_heads, local_width)[None, None]
    resp_dq = mine[..., q_width : 2 * q_width].reshape(
        peers, resp_len, kv_heads, local_width
    )[None, None]
    resp_dkv = jnp.moveaxis(
        mine[..., 2 * q_width :].reshape(peers, resp_len, 2, kv_width // 2), 2, 0
    )[:, None, None]
    prompt_out = out[peers:]
    prompt_dq = dq[peers:]
    return (prompt_out, prompt_dq, prompt_dkv, resp_out, resp_dq, resp_dkv)


def solution(mesh):
    return jax.shard_map(
        body,
        mesh=mesh,
        in_specs=(
            P("resp", "prompt", None, "head"),
            P(None, "resp", "prompt", None),
            P("resp", "prompt", None, "head"),
            P("prompt", "resp", None, None, None, "head"),
            P(None, "prompt", "resp", None, None, None),
            P("prompt", "resp", None, None, None, "head"),
            P("prompt", "resp", None),
        ),
        out_specs=(
            P("resp", "prompt", None, "head"),
            P("resp", "prompt", None, "head"),
            P(None, "resp", "prompt", "head"),
            P("prompt", "resp", None, None, None, "head"),
            P("prompt", "resp", None, None, None, "head"),
            P(None, "prompt", "resp", None, None, "head"),
        ),
        check_vma=False,
    )
```

```python
import math

import jax
import jax.numpy as jnp
from jax import lax
from jax.sharding import PartitionSpec as P

HD = 128


def attend_blocks(queries, keys_in, values_in, own_keys, own_values, cotangent, shared_ok, own_ok):
    scale = 1.0 / math.sqrt(HD)
    f32 = jnp.float32
    s_sh = jnp.einsum("brkgd,nkd->bkgrn", queries, keys_in, preferred_element_type=f32) * scale
    s_own = jnp.einsum("brkgd,bukd->bkgru", queries, own_keys, preferred_element_type=f32) * scale
    s_sh = jnp.where(shared_ok[:, None, None], s_sh, -1e30)
    s_own = jnp.where(own_ok[:, None, None], s_own, -1e30)
    row_max = jnp.maximum(
        jnp.max(s_sh, axis=-1, keepdims=True), jnp.max(s_own, axis=-1, keepdims=True)
    )
    totals = jnp.sum(jnp.exp(s_sh - row_max), axis=-1, keepdims=True) + jnp.sum(
        jnp.exp(s_own - row_max), axis=-1, keepdims=True
    )
    log_total = row_max + jnp.log(totals)
    p_sh = jnp.exp(s_sh - log_total)
    p_own = jnp.exp(s_own - log_total)
    w_sh = p_sh.astype(jnp.bfloat16)
    w_own = p_own.astype(jnp.bfloat16)
    output = (
        jnp.einsum("bkgrn,nkd->brkgd", w_sh, values_in, preferred_element_type=f32)
        + jnp.einsum("bkgru,bukd->brkgd", w_own, own_values, preferred_element_type=f32)
    ).astype(jnp.bfloat16)
    row_delta = jnp.einsum("brkgd,brkgd->bkgr", cotangent, output, preferred_element_type=f32)
    dp_sh = jnp.einsum("brkgd,nkd->bkgrn", cotangent, values_in, preferred_element_type=f32)
    dp_own = jnp.einsum("brkgd,bukd->bkgru", cotangent, own_values, preferred_element_type=f32)
    ds_sh = (p_sh * (dp_sh - row_delta[..., None])).astype(jnp.bfloat16)
    ds_own = (p_own * (dp_own - row_delta[..., None])).astype(jnp.bfloat16)
    dquery = (
        jnp.einsum("bkgrn,nkd->brkgd", ds_sh, keys_in, preferred_element_type=f32)
        + jnp.einsum("bkgru,bukd->brkgd", ds_own, own_keys, preferred_element_type=f32)
    ) * scale
    dk_sh = jnp.einsum("bkgrn,brkgd->knd", ds_sh, queries, preferred_element_type=f32) * scale
    dv_sh = jnp.einsum("bkgrn,brkgd->knd", w_sh, cotangent, preferred_element_type=f32)
    dk_own = jnp.einsum("bkgru,brkgd->kbud", ds_own, queries, preferred_element_type=f32) * scale
    dv_own = jnp.einsum("bkgru,brkgd->kbud", w_own, cotangent, preferred_element_type=f32)
    return output, dquery, dk_sh, dv_sh, dk_own, dv_own


def scatter_sum(x, axis_name, dim):
    n = lax.axis_size(axis_name)
    got = lax.all_to_all(x, axis_name, split_axis=dim, concat_axis=dim, tiled=True)
    shape = x.shape[:dim] + (n, x.shape[dim] // n) + x.shape[dim + 1 :]
    return jnp.sum(got.reshape(shape), axis=dim)


def all_gather_by_all_to_all(x, axis_name):
    n = lax.axis_size(axis_name)
    repeated = jnp.broadcast_to(x[None], (n,) + x.shape)
    return lax.all_to_all(repeated, axis_name, split_axis=0, concat_axis=0, tiled=True).reshape(
        (n * x.shape[0],) + x.shape[1:]
    )


def swap_sum(x):
    core = lax.axis_index("head")
    half = x.shape[0] // 2
    mine = lax.dynamic_slice_in_dim(x, core * half, half, axis=0)
    theirs = lax.dynamic_slice_in_dim(x, (1 - core) * half, half, axis=0)
    return mine + lax.ppermute(theirs, "head", [(0, 1), (1, 0)])


def body(prompt_q, prompt_kv, prompt_grad, resp_q, resp_kv, resp_grad, resp_prompt):
    head_size = HD
    block_rows = prompt_q.shape[1]
    kv_heads = prompt_q.shape[2]
    local_width = prompt_q.shape[3]
    local_heads = local_width // head_size
    full_len = block_rows * lax.axis_size("prompt")
    resp_len = resp_q.shape[3]
    peers = lax.axis_size("resp")
    kv_width = kv_heads * head_size
    q_width = kv_heads * local_width
    half = lax.dynamic_index_in_dim(prompt_kv[:, 0], lax.axis_index("head"), 0, keepdims=False)
    gathered_half = all_gather_by_all_to_all(half, "prompt")
    other_half = lax.ppermute(gathered_half, "head", [(0, 1), (1, 0)])
    on_core0 = lax.axis_index("head") == 0
    prompt_keys = jnp.where(on_core0, gathered_half, other_half).reshape(full_len, kv_heads, head_size)
    prompt_values = jnp.where(on_core0, other_half, gathered_half).reshape(
        full_len, kv_heads, head_size
    )

    order = resp_prompt[0, 0]
    picker = (jnp.arange(peers)[:, None] == order[None, :]).astype(jnp.bfloat16)
    stacked = jnp.concatenate(
        [
            resp_q[0, 0].reshape(peers, resp_len, q_width),
            jnp.moveaxis(resp_kv[:, 0, 0], 0, 2).reshape(peers, resp_len, 2 * kv_width),
            resp_grad[0, 0].reshape(peers, resp_len, q_width),
        ],
        axis=-1,
    )
    send = jnp.einsum(
        "dj,jrh->drh", picker, stacked, preferred_element_type=jnp.float32
    ).astype(jnp.bfloat16)
    got = lax.all_to_all(send, "resp", split_axis=0, concat_axis=0, tiled=True)
    got_q = got[..., :q_width]
    got_kv = jnp.moveaxis(
        got[..., q_width : q_width + 2 * kv_width].reshape(peers, resp_len, 2, kv_width), 2, 1
    )
    got_grad = got[..., q_width + 2 * kv_width :]

    q_shape = (peers + 1, resp_len, kv_heads, local_heads, head_size)
    queries = jnp.concatenate([got_q, prompt_q[0].reshape(1, resp_len, q_width)], axis=0).reshape(q_shape)
    cotangent = jnp.concatenate([got_grad, prompt_grad[0].reshape(1, resp_len, q_width)], axis=0).reshape(q_shape)
    own_kv = jnp.concatenate(
        [got_kv, jnp.zeros((1,) + got_kv.shape[1:], got_kv.dtype)], axis=0
    ).reshape(peers + 1, 2, resp_len, kv_heads, head_size)
    query_rows = lax.axis_index("prompt") * block_rows + jnp.arange(block_rows)
    key_cols = jnp.arange(full_len)
    causal = key_cols[None, :] <= query_rows[:, None]
    shared_ok = jnp.concatenate(
        [jnp.ones((peers, resp_len, full_len), bool), causal[None]], axis=0
    )
    steps_own = jnp.arange(resp_len)
    own_causal = steps_own[None, :] <= steps_own[:, None]
    own_ok = jnp.concatenate(
        [
            jnp.broadcast_to(own_causal, (peers, resp_len, resp_len)),
            jnp.zeros((1, resp_len, resp_len), bool),
        ],
        axis=0,
    )
    out, dq, dk_sh, dv_sh, dk_own, dv_own = attend_blocks(
        queries,
        prompt_keys,
        prompt_values,
        own_kv[:, 0],
        own_kv[:, 1],
        cotangent,
        shared_ok,
        own_ok,
    )
    out = out.reshape(peers + 1, resp_len, kv_heads, local_width)
    dq = dq.astype(jnp.bfloat16).reshape(peers + 1, resp_len, kv_heads, local_width)

    n_blocks = lax.axis_size("prompt")
    local_kv = kv_heads // lax.axis_size("head")

    both_parts = jnp.stack([dk_sh, dv_sh], axis=1)
    mine = swap_sum(both_parts).reshape(local_kv, 2, n_blocks, block_rows, head_size)
    got_blocks = lax.all_to_all(
        jnp.moveaxis(mine, 2, 0), "prompt", split_axis=0, concat_axis=0, tiled=True
    )
    total = jnp.sum(got_blocks, axis=0)
    block_sum = jnp.transpose(total, (1, 2, 0, 3)).reshape(2, block_rows, local_kv * head_size)
    own_sum = swap_sum(jnp.stack([dk_own[:, :peers], dv_own[:, :peers]], axis=1))
    back_kv = (
        jnp.transpose(own_sum, (2, 3, 1, 0, 4))
        .reshape(peers, resp_len, 2 * local_kv * head_size)
        .astype(jnp.bfloat16)
    )
    prompt_dkv = block_sum.astype(jnp.bfloat16)[:, None]
    back = jnp.concatenate(
        [
            out[:peers].reshape(peers, resp_len, q_width),
            dq[:peers].reshape(peers, resp_len, q_width),
            back_kv,
        ],
        axis=-1,
    )
    ret = lax.all_to_all(back, "resp", split_axis=0, concat_axis=0, tiled=True)
    mine = jnp.einsum(
        "dj,drh->jrh", picker, ret, preferred_element_type=jnp.float32
    ).astype(jnp.bfloat16)
    resp_out = mine[..., :q_width].reshape(peers, resp_len, kv_heads, local_width)[None, None]
    resp_dq = mine[..., q_width : 2 * q_width].reshape(
        peers, resp_len, kv_heads, local_width
    )[None, None]
    resp_dkv = jnp.moveaxis(
        mine[..., 2 * q_width :].reshape(peers, resp_len, 2, kv_width // 2), 2, 0
    )[:, None, None]
    prompt_out = out[peers:]
    prompt_dq = dq[peers:]
    return (prompt_out, prompt_dq, prompt_dkv, resp_out, resp_dq, resp_dkv)


def solution(mesh):
    return jax.shard_map(
        body,
        mesh=mesh,
        in_specs=(
            P("resp", "prompt", None, "head"),
            P(None, "resp", "prompt", None),
            P("resp", "prompt", None, "head"),
            P("prompt", "resp", None, None, None, "head"),
            P(None, "prompt", "resp", None, None, None),
            P("prompt", "resp", None, None, None, "head"),
            P("prompt", "resp", None),
        ),
        out_specs=(
            P("resp", "prompt", None, "head"),
            P("resp", "prompt", None, "head"),
            P(None, "resp", "prompt", "head"),
            P("prompt", "resp", None, None, None, "head"),
            P("prompt", "resp", None, None, None, "head"),
            P(None, "prompt", "resp", None, None, "head"),
        ),
        check_vma=False,
    )
```

```python
import math

import jax
import jax.numpy as jnp
from jax import lax
from jax.sharding import PartitionSpec as P

HD = 128


def attend_blocks(queries, keys_in, values_in, own_keys, own_values, cotangent, shared_ok, own_ok):
    scale = 1.0 / math.sqrt(HD)
    f32 = jnp.float32
    s_sh = jnp.einsum("brkgd,nkd->bkgrn", queries, keys_in, preferred_element_type=f32) * scale
    s_own = jnp.einsum("brkgd,bukd->bkgru", queries, own_keys, preferred_element_type=f32) * scale
    s_sh = jnp.where(shared_ok[:, None, None], s_sh, -1e30)
    s_own = jnp.where(own_ok[:, None, None], s_own, -1e30)
    row_max = jnp.maximum(
        jnp.max(s_sh, axis=-1, keepdims=True), jnp.max(s_own, axis=-1, keepdims=True)
    )
    totals = jnp.sum(jnp.exp(s_sh - row_max), axis=-1, keepdims=True) + jnp.sum(
        jnp.exp(s_own - row_max), axis=-1, keepdims=True
    )
    log_total = row_max + jnp.log(totals)
    p_sh = jnp.exp(s_sh - log_total)
    p_own = jnp.exp(s_own - log_total)
    w_sh = p_sh.astype(jnp.bfloat16)
    w_own = p_own.astype(jnp.bfloat16)
    output = (
        jnp.einsum("bkgrn,nkd->brkgd", w_sh, values_in, preferred_element_type=f32)
        + jnp.einsum("bkgru,bukd->brkgd", w_own, own_values, preferred_element_type=f32)
    ).astype(jnp.bfloat16)
    row_delta = jnp.einsum("brkgd,brkgd->bkgr", cotangent, output, preferred_element_type=f32)
    dp_sh = jnp.einsum("brkgd,nkd->bkgrn", cotangent, values_in, preferred_element_type=f32)
    dp_own = jnp.einsum("brkgd,bukd->bkgru", cotangent, own_values, preferred_element_type=f32)
    ds_sh = (p_sh * (dp_sh - row_delta[..., None])).astype(jnp.bfloat16)
    ds_own = (p_own * (dp_own - row_delta[..., None])).astype(jnp.bfloat16)
    dquery = (
        jnp.einsum("bkgrn,nkd->brkgd", ds_sh, keys_in, preferred_element_type=f32)
        + jnp.einsum("bkgru,bukd->brkgd", ds_own, own_keys, preferred_element_type=f32)
    ) * scale
    dk_sh = jnp.einsum("bkgrn,brkgd->knd", ds_sh, queries, preferred_element_type=f32) * scale
    dv_sh = jnp.einsum("bkgrn,brkgd->knd", w_sh, cotangent, preferred_element_type=f32)
    dk_own = jnp.einsum("bkgru,brkgd->kbud", ds_own, queries, preferred_element_type=f32) * scale
    dv_own = jnp.einsum("bkgru,brkgd->kbud", w_own, cotangent, preferred_element_type=f32)
    return output, dquery, dk_sh, dv_sh, dk_own, dv_own


def scatter_sum(x, axis_name, dim):
    n = lax.axis_size(axis_name)
    got = lax.all_to_all(x, axis_name, split_axis=dim, concat_axis=dim, tiled=True)
    shape = x.shape[:dim] + (n, x.shape[dim] // n) + x.shape[dim + 1 :]
    return jnp.sum(got.reshape(shape), axis=dim)


def all_gather_by_all_to_all(x, axis_name):
    n = lax.axis_size(axis_name)
    repeated = jnp.broadcast_to(x[None], (n,) + x.shape)
    return lax.all_to_all(repeated, axis_name, split_axis=0, concat_axis=0, tiled=True).reshape(
        (n * x.shape[0],) + x.shape[1:]
    )


def swap_sum(x):
    core = lax.axis_index("head")
    half = x.shape[0] // 2
    mine = lax.dynamic_slice_in_dim(x, core * half, half, axis=0)
    theirs = lax.dynamic_slice_in_dim(x, (1 - core) * half, half, axis=0)
    return mine + lax.ppermute(theirs, "head", [(0, 1), (1, 0)])


def body(prompt_q, prompt_kv, prompt_grad, resp_q, resp_kv, resp_grad, resp_prompt):
    head_size = HD
    block_rows = prompt_q.shape[1]
    kv_heads = prompt_q.shape[2]
    local_width = prompt_q.shape[3]
    local_heads = local_width // head_size
    full_len = block_rows * lax.axis_size("prompt")
    resp_len = resp_q.shape[3]
    peers = lax.axis_size("resp")
    kv_width = kv_heads * head_size
    q_width = kv_heads * local_width
    half = lax.dynamic_index_in_dim(prompt_kv[:, 0], lax.axis_index("head"), 0, keepdims=False)
    gathered_half = all_gather_by_all_to_all(half, "prompt")
    other_half = lax.ppermute(gathered_half, "head", [(0, 1), (1, 0)])
    on_core0 = lax.axis_index("head") == 0
    prompt_keys = jnp.where(on_core0, gathered_half, other_half).reshape(full_len, kv_heads, head_size)
    prompt_values = jnp.where(on_core0, other_half, gathered_half).reshape(
        full_len, kv_heads, head_size
    )

    order = resp_prompt[0, 0]
    picker = (jnp.arange(peers)[:, None] == order[None, :]).astype(jnp.bfloat16)
    stacked = jnp.concatenate(
        [
            resp_q[0, 0].reshape(peers, resp_len, q_width),
            lax.dynamic_index_in_dim(resp_kv[:, 0, 0], lax.axis_index("head"), 0, keepdims=False),
            resp_grad[0, 0].reshape(peers, resp_len, q_width),
        ],
        axis=-1,
    )
    send = jnp.einsum(
        "dj,jrh->drh", picker, stacked, preferred_element_type=jnp.float32
    ).astype(jnp.bfloat16)
    got = lax.all_to_all(send, "resp", split_axis=0, concat_axis=0, tiled=True)
    got_q = got[..., :q_width]
    got_half = got[..., q_width : q_width + kv_width]
    other_got = lax.ppermute(got_half, "head", [(0, 1), (1, 0)])
    got_kv = jnp.stack(
        [jnp.where(on_core0, got_half, other_got), jnp.where(on_core0, other_got, got_half)], axis=1
    )
    got_grad = got[..., q_width + kv_width :]

    q_shape = (peers + 1, resp_len, kv_heads, local_heads, head_size)
    queries = jnp.concatenate([got_q, prompt_q[0].reshape(1, resp_len, q_width)], axis=0).reshape(q_shape)
    cotangent = jnp.concatenate([got_grad, prompt_grad[0].reshape(1, resp_len, q_width)], axis=0).reshape(q_shape)
    own_kv = jnp.concatenate(
        [got_kv, jnp.zeros((1,) + got_kv.shape[1:], got_kv.dtype)], axis=0
    ).reshape(peers + 1, 2, resp_len, kv_heads, head_size)
    query_rows = lax.axis_index("prompt") * block_rows + jnp.arange(block_rows)
    key_cols = jnp.arange(full_len)
    causal = key_cols[None, :] <= query_rows[:, None]
    shared_ok = jnp.concatenate(
        [jnp.ones((peers, resp_len, full_len), bool), causal[None]], axis=0
    )
    steps_own = jnp.arange(resp_len)
    own_causal = steps_own[None, :] <= steps_own[:, None]
    own_ok = jnp.concatenate(
        [
            jnp.broadcast_to(own_causal, (peers, resp_len, resp_len)),
            jnp.zeros((1, resp_len, resp_len), bool),
        ],
        axis=0,
    )
    out, dq, dk_sh, dv_sh, dk_own, dv_own = attend_blocks(
        queries,
        prompt_keys,
        prompt_values,
        own_kv[:, 0],
        own_kv[:, 1],
        cotangent,
        shared_ok,
        own_ok,
    )
    out = out.reshape(peers + 1, resp_len, kv_heads, local_width)
    dq = dq.astype(jnp.bfloat16).reshape(peers + 1, resp_len, kv_heads, local_width)

    n_blocks = lax.axis_size("prompt")
    local_kv = kv_heads // lax.axis_size("head")

    both_parts = jnp.stack([dk_sh, dv_sh], axis=1)
    mine = swap_sum(both_parts).reshape(local_kv, 2, n_blocks, block_rows, head_size)
    got_blocks = lax.all_to_all(
        jnp.moveaxis(mine, 2, 0), "prompt", split_axis=0, concat_axis=0, tiled=True
    )
    total = jnp.sum(got_blocks, axis=0)
    block_sum = jnp.transpose(total, (1, 2, 0, 3)).reshape(2, block_rows, local_kv * head_size)
    own_sum = swap_sum(jnp.stack([dk_own[:, :peers], dv_own[:, :peers]], axis=1))
    back_kv = (
        jnp.transpose(own_sum, (2, 3, 1, 0, 4))
        .reshape(peers, resp_len, 2 * local_kv * head_size)
        .astype(jnp.bfloat16)
    )
    prompt_dkv = block_sum.astype(jnp.bfloat16)[:, None]
    back = jnp.concatenate(
        [
            out[:peers].reshape(peers, resp_len, q_width),
            dq[:peers].reshape(peers, resp_len, q_width),
            back_kv,
        ],
        axis=-1,
    )
    ret = lax.all_to_all(back, "resp", split_axis=0, concat_axis=0, tiled=True)
    mine = jnp.einsum(
        "dj,drh->jrh", picker, ret, preferred_element_type=jnp.float32
    ).astype(jnp.bfloat16)
    resp_out = mine[..., :q_width].reshape(peers, resp_len, kv_heads, local_width)[None, None]
    resp_dq = mine[..., q_width : 2 * q_width].reshape(
        peers, resp_len, kv_heads, local_width
    )[None, None]
    resp_dkv = jnp.moveaxis(
        mine[..., 2 * q_width :].reshape(peers, resp_len, 2, kv_width // 2), 2, 0
    )[:, None, None]
    prompt_out = out[peers:]
    prompt_dq = dq[peers:]
    return (prompt_out, prompt_dq, prompt_dkv, resp_out, resp_dq, resp_dkv)


def solution(mesh):
    return jax.shard_map(
        body,
        mesh=mesh,
        in_specs=(
            P("resp", "prompt", None, "head"),
            P(None, "resp", "prompt", None),
            P("resp", "prompt", None, "head"),
            P("prompt", "resp", None, None, None, "head"),
            P(None, "prompt", "resp", None, None, None),
            P("prompt", "resp", None, None, None, "head"),
            P("prompt", "resp", None),
        ),
        out_specs=(
            P("resp", "prompt", None, "head"),
            P("resp", "prompt", None, "head"),
            P(None, "resp", "prompt", "head"),
            P("prompt", "resp", None, None, None, "head"),
            P("prompt", "resp", None, None, None, "head"),
            P(None, "prompt", "resp", None, None, "head"),
        ),
        check_vma=False,
    )
```

```python
import math

import jax
import jax.numpy as jnp
from jax import lax
from jax.sharding import PartitionSpec as P

HD = 128


def attend_blocks(
    queries, keys_in, values_in, own_keys, own_values, cotangent, shared_limit, own_limit
):
    scale = 1.0 / math.sqrt(HD)
    f32 = jnp.float32
    s_sh = jnp.einsum("brkgd,nkd->bkgrn", queries, keys_in, preferred_element_type=f32) * scale
    s_own = jnp.einsum("brkgd,bukd->bkgru", queries, own_keys, preferred_element_type=f32) * scale
    shared_ok = lax.broadcasted_iota(jnp.int32, s_sh.shape, 4) <= shared_limit[:, None, None, :, None]
    own_ok = lax.broadcasted_iota(jnp.int32, s_own.shape, 4) <= own_limit[:, None, None, :, None]
    s_sh = jnp.where(shared_ok, s_sh, -1e30)
    s_own = jnp.where(own_ok, s_own, -1e30)
    row_max = jnp.maximum(
        jnp.max(s_sh, axis=-1, keepdims=True), jnp.max(s_own, axis=-1, keepdims=True)
    )
    totals = jnp.sum(jnp.exp(s_sh - row_max), axis=-1, keepdims=True) + jnp.sum(
        jnp.exp(s_own - row_max), axis=-1, keepdims=True
    )
    log_total = row_max + jnp.log(totals)
    p_sh = jnp.exp(s_sh - log_total)
    p_own = jnp.exp(s_own - log_total)
    w_sh = p_sh.astype(jnp.bfloat16)
    w_own = p_own.astype(jnp.bfloat16)
    output = (
        jnp.einsum("bkgrn,nkd->brkgd", w_sh, values_in, preferred_element_type=f32)
        + jnp.einsum("bkgru,bukd->brkgd", w_own, own_values, preferred_element_type=f32)
    ).astype(jnp.bfloat16)
    row_delta = jnp.einsum("brkgd,brkgd->bkgr", cotangent, output, preferred_element_type=f32)
    dp_sh = jnp.einsum("brkgd,nkd->bkgrn", cotangent, values_in, preferred_element_type=f32)
    dp_own = jnp.einsum("brkgd,bukd->bkgru", cotangent, own_values, preferred_element_type=f32)
    ds_sh = (p_sh * (dp_sh - row_delta[..., None])).astype(jnp.bfloat16)
    ds_own = (p_own * (dp_own - row_delta[..., None])).astype(jnp.bfloat16)
    dquery = (
        jnp.einsum("bkgrn,nkd->brkgd", ds_sh, keys_in, preferred_element_type=f32)
        + jnp.einsum("bkgru,bukd->brkgd", ds_own, own_keys, preferred_element_type=f32)
    ) * scale
    dk_sh = jnp.einsum("bkgrn,brkgd->knd", ds_sh, queries, preferred_element_type=f32) * scale
    dv_sh = jnp.einsum("bkgrn,brkgd->knd", w_sh, cotangent, preferred_element_type=f32)
    dk_own = jnp.einsum("bkgru,brkgd->kbud", ds_own, queries, preferred_element_type=f32) * scale
    dv_own = jnp.einsum("bkgru,brkgd->kbud", w_own, cotangent, preferred_element_type=f32)
    return output, dquery, dk_sh, dv_sh, dk_own, dv_own


def scatter_sum(x, axis_name, dim):
    n = lax.axis_size(axis_name)
    got = lax.all_to_all(x, axis_name, split_axis=dim, concat_axis=dim, tiled=True)
    shape = x.shape[:dim] + (n, x.shape[dim] // n) + x.shape[dim + 1 :]
    return jnp.sum(got.reshape(shape), axis=dim)


def all_gather_by_all_to_all(x, axis_name):
    n = lax.axis_size(axis_name)
    repeated = jnp.broadcast_to(x[None], (n,) + x.shape)
    return lax.all_to_all(repeated, axis_name, split_axis=0, concat_axis=0, tiled=True).reshape(
        (n * x.shape[0],) + x.shape[1:]
    )


def swap_sum(x):
    core = lax.axis_index("head")
    half = x.shape[0] // 2
    mine = lax.dynamic_slice_in_dim(x, core * half, half, axis=0)
    theirs = lax.dynamic_slice_in_dim(x, (1 - core) * half, half, axis=0)
    return mine + lax.ppermute(theirs, "head", [(0, 1), (1, 0)])


def body(prompt_q, prompt_kv, prompt_grad, resp_q, resp_kv, resp_grad, resp_prompt):
    head_size = HD
    block_rows = prompt_q.shape[1]
    kv_heads = prompt_q.shape[2]
    local_width = prompt_q.shape[3]
    local_heads = local_width // head_size
    full_len = block_rows * lax.axis_size("prompt")
    resp_len = resp_q.shape[3]
    peers = lax.axis_size("resp")
    kv_width = kv_heads * head_size
    q_width = kv_heads * local_width
    half = lax.dynamic_index_in_dim(prompt_kv[:, 0], lax.axis_index("head"), 0, keepdims=False)
    gathered_half = all_gather_by_all_to_all(half, "prompt")
    other_half = lax.ppermute(gathered_half, "head", [(0, 1), (1, 0)])
    on_core0 = lax.axis_index("head") == 0
    prompt_keys = jnp.where(on_core0, gathered_half, other_half).reshape(full_len, kv_heads, head_size)
    prompt_values = jnp.where(on_core0, other_half, gathered_half).reshape(
        full_len, kv_heads, head_size
    )

    order = resp_prompt[0, 0]
    picker = (jnp.arange(peers)[:, None] == order[None, :]).astype(jnp.bfloat16)
    stacked = jnp.concatenate(
        [
            resp_q[0, 0].reshape(peers, resp_len, q_width),
            lax.dynamic_index_in_dim(resp_kv[:, 0, 0], lax.axis_index("head"), 0, keepdims=False),
            resp_grad[0, 0].reshape(peers, resp_len, q_width),
        ],
        axis=-1,
    )
    send = jnp.einsum(
        "dj,jrh->drh", picker, stacked, preferred_element_type=jnp.float32
    ).astype(jnp.bfloat16)
    got = lax.all_to_all(send, "resp", split_axis=0, concat_axis=0, tiled=True)
    got_q = got[..., :q_width]
    got_half = got[..., q_width : q_width + kv_width]
    other_got = lax.ppermute(got_half, "head", [(0, 1), (1, 0)])
    got_kv = jnp.stack(
        [jnp.where(on_core0, got_half, other_got), jnp.where(on_core0, other_got, got_half)], axis=1
    )
    got_grad = got[..., q_width + kv_width :]

    q_shape = (peers + 1, resp_len, kv_heads, local_heads, head_size)
    queries = jnp.concatenate([got_q, prompt_q[0].reshape(1, resp_len, q_width)], axis=0).reshape(q_shape)
    cotangent = jnp.concatenate([got_grad, prompt_grad[0].reshape(1, resp_len, q_width)], axis=0).reshape(q_shape)
    own_kv = jnp.concatenate(
        [got_kv, jnp.zeros((1,) + got_kv.shape[1:], got_kv.dtype)], axis=0
    ).reshape(peers + 1, 2, resp_len, kv_heads, head_size)
    query_rows = lax.axis_index("prompt") * block_rows + jnp.arange(block_rows)
    steps_own = jnp.arange(resp_len)
    shared_limit = jnp.concatenate(
        [jnp.full((peers, resp_len), full_len, jnp.int32), query_rows[None].astype(jnp.int32)]
    )
    own_limit = jnp.concatenate(
        [
            jnp.broadcast_to(steps_own, (peers, resp_len)).astype(jnp.int32),
            jnp.full((1, resp_len), -1, jnp.int32),
        ]
    )
    out, dq, dk_sh, dv_sh, dk_own, dv_own = attend_blocks(
        queries,
        prompt_keys,
        prompt_values,
        own_kv[:, 0],
        own_kv[:, 1],
        cotangent,
        shared_limit,
        own_limit,
    )
    out = out.reshape(peers + 1, resp_len, kv_heads, local_width)
    dq = dq.astype(jnp.bfloat16).reshape(peers + 1, resp_len, kv_heads, local_width)

    n_blocks = lax.axis_size("prompt")
    local_kv = kv_heads // lax.axis_size("head")

    both_parts = jnp.stack([dk_sh, dv_sh], axis=1)
    mine = swap_sum(both_parts).reshape(local_kv, 2, n_blocks, block_rows, head_size)
    got_blocks = lax.all_to_all(
        jnp.moveaxis(mine, 2, 0), "prompt", split_axis=0, concat_axis=0, tiled=True
    )
    total = jnp.sum(got_blocks, axis=0)
    block_sum = jnp.transpose(total, (1, 2, 0, 3)).reshape(2, block_rows, local_kv * head_size)
    own_sum = swap_sum(jnp.stack([dk_own[:, :peers], dv_own[:, :peers]], axis=1))
    back_kv = (
        jnp.transpose(own_sum, (2, 3, 1, 0, 4))
        .reshape(peers, resp_len, 2 * local_kv * head_size)
        .astype(jnp.bfloat16)
    )
    prompt_dkv = block_sum.astype(jnp.bfloat16)[:, None]
    back = jnp.concatenate(
        [
            out[:peers].reshape(peers, resp_len, q_width),
            dq[:peers].reshape(peers, resp_len, q_width),
            back_kv,
        ],
        axis=-1,
    )
    ret = lax.all_to_all(back, "resp", split_axis=0, concat_axis=0, tiled=True)
    mine = jnp.einsum(
        "dj,drh->jrh", picker, ret, preferred_element_type=jnp.float32
    ).astype(jnp.bfloat16)
    resp_out = mine[..., :q_width].reshape(peers, resp_len, kv_heads, local_width)[None, None]
    resp_dq = mine[..., q_width : 2 * q_width].reshape(
        peers, resp_len, kv_heads, local_width
    )[None, None]
    resp_dkv = jnp.moveaxis(
        mine[..., 2 * q_width :].reshape(peers, resp_len, 2, kv_width // 2), 2, 0
    )[:, None, None]
    prompt_out = out[peers:]
    prompt_dq = dq[peers:]
    return (prompt_out, prompt_dq, prompt_dkv, resp_out, resp_dq, resp_dkv)


def solution(mesh):
    return jax.shard_map(
        body,
        mesh=mesh,
        in_specs=(
            P("resp", "prompt", None, "head"),
            P(None, "resp", "prompt", None),
            P("resp", "prompt", None, "head"),
            P("prompt", "resp", None, None, None, "head"),
            P(None, "prompt", "resp", None, None, None),
            P("prompt", "resp", None, None, None, "head"),
            P("prompt", "resp", None),
        ),
        out_specs=(
            P("resp", "prompt", None, "head"),
            P("resp", "prompt", None, "head"),
            P(None, "resp", "prompt", "head"),
            P("prompt", "resp", None, None, None, "head"),
            P("prompt", "resp", None, None, None, "head"),
            P(None, "prompt", "resp", None, None, "head"),
        ),
        check_vma=False,
    )
```
